512 devices in a mesh: ctx: 64 (over z, y_lo, core), head: 8 (over x, y_hi).
Axes of the slice: x: 4, y: 4 (y_hi: 2, y_lo: 2; y = y_hi * 2 + y_lo), z: 16, core: 2. Of those that a mesh axis runs over, the one named last changes fastest.
Arguments:
- queries_nope: bfloat16 [4096, 8192], P('ctx', 'head'), may hold values from -4 to 4
- queries_rope: bfloat16 [4096, 4096], P('ctx', 'head'), may hold values from -128 to 128
- latents: bfloat16 [4096, 512], P('ctx'), may hold values from -8 to 8
- rope_keys: bfloat16 [4096, 64], P('ctx'), may hold values from -4 to 4
- positions: int32 [4096], P('ctx'), may hold values from 0 to 6143
- key_up: bfloat16 [512, 8192], P(None, 'head'), may hold values from -0.5 to 0.5
- value_up: bfloat16 [512, 8192], P(None, 'head'), may hold values from -0.25 to 0.25
- out_proj: bfloat16 [8192, 3584], P('head', 'ctx'), may hold values from -0.0625 to 0.0625
Outputs:
- attended: bfloat16 [4096, 3584], P('ctx', 'head')
The draws below stay inside these ranges and needn't reach their ends.
All inputs are finite; a program needn't handle non-finite values.
Results may differ from the reference program's by a relative error of at most 0.014.
The reference program's roundings to bfloat16 on the way count: a program that leaves them out, or rounds other values in their place, can miss the bound.
Values may be sent and summed in bfloat16 or wider, within the bound.
No kernel may reach another device: no remote copies, remote signals or barrier semaphores. Data moves between devices by JAX's collectives and lax.ppermute only.
A program may use at most 64 MiB of HBM per device.

```python
import math
import jax
import jax.numpy as jnp
from jax import lax

LATENT = 512
ROPE = 64
NOPE = 128
VDIM = 128
H = 64
DOUT = 3584
TOKENS = 4096


def draw_queries_nope(key, part):
    draw_key = jax.random.fold_in(key, 21)
    values = jnp.clip(jax.random.normal(draw_key, (TOKENS, H * NOPE)), -4.0, 4.0)
    return values.astype(jnp.bfloat16)


def draw_queries_rope(key, part):
    draw_key = jax.random.fold_in(key, 22)
    values = jnp.clip(jax.random.normal(draw_key, (TOKENS, H * ROPE)), -4.0, 4.0)
    return values.astype(jnp.bfloat16)


def draw_rope_keys(key, part):
    draw_key = jax.random.fold_in(key, 23)
    values = jnp.clip(jax.random.normal(draw_key, (TOKENS, ROPE)), -4.0, 4.0)
    return values.astype(jnp.bfloat16)


def draw_positions(key, part):
    order = jax.random.permutation(jax.random.fold_in(key, 24), TOKENS - 1)
    gaps = jnp.where(order < TOKENS // 2, 2, 1).astype(jnp.int32)
    start = jnp.zeros((1,), jnp.int32)
    return jnp.concatenate([start, jnp.cumsum(gaps).astype(jnp.int32)]).astype(jnp.int32)


def levels(key, extent, cuts, least, top_value):
    def one(position, blocks):
        draws = jax.random.uniform(jax.random.fold_in(jax.random.fold_in(key, 6), position), (blocks,), jnp.float32, least / len(cuts), top_value / len(cuts))
        return jnp.repeat(jnp.exp(draws), extent[position] // blocks).reshape((-1,) + (1,) * (len(extent) - position - 1))

    factor_of = one(*cuts[0])
    for cut in cuts[1:]:
        factor_of = factor_of * one(*cut)
    return factor_of


def noise(own_key, extent, scale, most, cuts=(), held_as=jnp.bfloat16):
    result = jax.random.normal(own_key, extent, jnp.float32) * scale
    if len(cuts) > 0:
        result = levels(own_key, extent, cuts, -0.22, 0.18) * result
    return jnp.clip(result, min=-most, max=most).astype(held_as)


def setup_inputs(seed: int = 0) -> dict:
    splits = jax.random.split(jax.random.key(seed), 9)
    return {
        "queries_nope": draw_queries_nope(jax.random.fold_in(splits[8], 71), 0),
        "queries_rope": draw_queries_rope(jax.random.fold_in(splits[8], 71), 0),
        "latents": noise(splits[2], (TOKENS, LATENT), 1.5, 8.0, ((0, 64),)),
        "rope_keys": draw_rope_keys(jax.random.fold_in(splits[8], 71), 0),
        "positions": draw_positions(jax.random.fold_in(splits[8], 71), 0),
        "key_up": noise(splits[5], (LATENT, H * NOPE), NOPE ** -0.5, 0.5, ((1, 8),)),
        "value_up": noise(splits[6], (LATENT, H * VDIM), LATENT ** -0.5, 0.25, ((1, 8),)),
        "out_proj": noise(splits[7], (H * VDIM, DOUT), (H * VDIM) ** -0.5, 0.0625, ((0, 8), (1, 64))),
    }


masked_value = -1e+30

def rope_tables(token_pos, width):
    half_width = width // 2
    freqs = jnp.exp(jnp.arange(half_width, dtype=jnp.float32) * (-2.0 * math.log(10000.0) / width))
    angle = token_pos.astype(jnp.float32)[:, None] * freqs[None, :]
    return (jnp.cos(angle), jnp.sin(angle))

def rotate(values, cosine, sine):
    half_width = values.shape[-1] // 2
    first_half = values[..., :half_width]
    second_half = values[..., half_width:]
    cos_part = cosine[:, None, :]
    sin_part = sine[:, None, :]
    return jnp.concatenate([first_half * cos_part - second_half * sin_part, second_half * cos_part + first_half * sin_part], axis=-1)

def reference(queries_nope, queries_rope, latents, rope_keys, positions, key_up, value_up, out_proj):
    scale = 1.0 / math.sqrt(NOPE + ROPE)
    cosine, sine = rope_tables(positions, ROPE)
    rot_queries = rotate(queries_rope.astype(jnp.float32).reshape(TOKENS, H, ROPE), cosine, sine).astype(jnp.bfloat16)
    rot_keys = rotate(rope_keys.astype(jnp.float32)[:, None, :], cosine, sine)[:, 0, :].astype(jnp.bfloat16)
    lat_queries = jnp.einsum('thn,lhn->thl', queries_nope.astype(jnp.float32).reshape(TOKENS, H, NOPE), key_up.astype(jnp.float32).reshape(LATENT, H, NOPE)).astype(jnp.bfloat16)
    visible = positions[None, :] <= positions[:, None]

    def one_head(index):
        lat_part = lat_queries[:, index, :]
        rope_part = rot_queries[:, index, :]
        scores = jnp.dot(lat_part, latents.T, preferred_element_type=jnp.float32) + jnp.dot(rope_part, rot_keys.T, preferred_element_type=jnp.float32)
        scores = jnp.where(visible, scores * scale, masked_value)
        peak = lax.optimization_barrier(jnp.max(scores, axis=1))
        weights = jnp.where(visible, jnp.exp(scores - peak[:, None]), 0.0)
        totals = lax.optimization_barrier(jnp.sum(weights, axis=1))
        summed = jnp.dot(weights.astype(jnp.bfloat16), latents, preferred_element_type=jnp.float32)
        return (summed / totals[:, None]).astype(jnp.bfloat16)
    latent_out = lax.map(one_head, jnp.arange(H))
    head_out = jnp.einsum('htl,lhd->thd', latent_out.astype(jnp.float32), value_up.astype(jnp.float32).reshape(LATENT, H, VDIM)).astype(jnp.bfloat16)
    head_out = head_out.reshape(TOKENS, H * VDIM)
    return jnp.dot(head_out, out_proj, preferred_element_type=jnp.float32).astype(jnp.bfloat16)
```

```python
import math

import jax
import jax.numpy as jnp
from jax import lax
from jax.sharding import PartitionSpec as P

LATENT = 512
ROPE = 64
NOPE = 128
VDIM = 128


masked_value = -1e30


def rope_tables(token_pos, width):
    half_width = width // 2
    freqs = jnp.exp(jnp.arange(half_width, dtype=jnp.float32) * (-2.0 * math.log(10000.0) / width))
    angle = token_pos.astype(jnp.float32)[:, None] * freqs[None, :]
    return (jnp.cos(angle), jnp.sin(angle))


def rotate(values, cosine, sine):
    half_width = values.shape[-1] // 2
    first_half = values[..., :half_width]
    second_half = values[..., half_width:]
    cos_part = cosine[:, None, :]
    sin_part = sine[:, None, :]
    return jnp.concatenate(
        [
            first_half * cos_part - second_half * sin_part,
            second_half * cos_part + first_half * sin_part,
        ],
        axis=-1,
    )


def attend(query_rows, query_index, keys, key_count):
    scale = 1.0 / math.sqrt(NOPE + ROPE)
    scores = jnp.einsum("rl,kl->rk", query_rows, keys, preferred_element_type=jnp.float32)
    key_index = lax.broadcasted_iota(jnp.int32, (1, key_count), 1)
    visible = key_index <= query_index[:, None]
    scores = jnp.where(visible, scores * scale, masked_value)
    peak = jnp.max(scores, axis=1)
    weights = jnp.where(visible, jnp.exp(scores - peak[:, None]), 0.0)
    totals = jnp.sum(weights, axis=1)
    summed = jnp.dot(
        weights.astype(jnp.bfloat16), keys[:, :LATENT], preferred_element_type=jnp.float32
    )
    return (summed / totals[:, None]).astype(jnp.bfloat16)


def upward(latent_out, value_up, token_count, head_count):
    head_out = jnp.einsum(
        "thl,lhd->thd",
        latent_out.reshape(token_count, head_count, LATENT),
        value_up.reshape(LATENT, head_count, VDIM),
        preferred_element_type=jnp.float32,
    )
    return head_out.astype(jnp.bfloat16).reshape(token_count, head_count * VDIM)


def body(queries_nope, queries_rope, latents, rope_keys, positions, key_up, value_up, out_proj):
    token_count = latents.shape[0]
    head_count = key_up.shape[1] // NOPE
    ctx_count = lax.axis_size("ctx")
    cosine, sine = rope_tables(positions, ROPE)
    rot_queries = rotate(
        queries_rope.astype(jnp.float32).reshape(token_count, head_count, ROPE), cosine, sine
    ).astype(jnp.bfloat16)
    rot_keys = rotate(rope_keys.astype(jnp.float32)[:, None, :], cosine, sine)[:, 0, :].astype(
        jnp.bfloat16
    )
    lat_queries = jnp.einsum(
        "thn,lhn->thl",
        queries_nope.reshape(token_count, head_count, NOPE),
        key_up.reshape(LATENT, head_count, NOPE),
        preferred_element_type=jnp.float32,
    ).astype(jnp.bfloat16)
    query_rows = jnp.concatenate([lat_queries, rot_queries], axis=-1).reshape(
        token_count * head_count, LATENT + ROPE
    )
    local_keys = jnp.concatenate([latents, rot_keys], axis=-1)
    keys = lax.all_gather(local_keys, "ctx", axis=0, tiled=True)
    first_token = lax.axis_index("ctx") * token_count
    query_index = jnp.repeat(
        first_token + jnp.arange(token_count, dtype=jnp.int32), head_count
    )
    latent_out = attend(query_rows, query_index, keys, token_count * ctx_count)
    head_out = upward(latent_out, value_up, token_count, head_count)
    partial_sums = jnp.dot(
        head_out,
        lax.all_gather(out_proj, "ctx", axis=1, tiled=True),
        preferred_element_type=jnp.float32,
    )
    return lax.psum_scatter(
        partial_sums.astype(jnp.bfloat16), "head", scatter_dimension=1, tiled=True
    )


def solution(mesh):
    in_specs = (
        P("ctx", "head"),
        P("ctx", "head"),
        P("ctx", None),
        P("ctx", None),
        P("ctx"),
        P(None, "head"),
        P(None, "head"),
        P("head", "ctx"),
    )
    out_specs = P("ctx", "head")
    return jax.shard_map(body, mesh=mesh, in_specs=in_specs, out_specs=out_specs, check_vma=False)
```

```python
import math

import jax
import jax.numpy as jnp
from jax import lax
from jax.sharding import Mesh
from jax.sharding import PartitionSpec as P

LATENT = 512
ROPE = 64
NOPE = 128
VDIM = 128


masked_value = -1e30


def rope_tables(token_pos, width):
    half_width = width // 2
    freqs = jnp.exp(jnp.arange(half_width, dtype=jnp.float32) * (-2.0 * math.log(10000.0) / width))
    angle = token_pos.astype(jnp.float32)[:, None] * freqs[None, :]
    return (jnp.cos(angle), jnp.sin(angle))


def rotate(values, cosine, sine):
    half_width = values.shape[-1] // 2
    first_half = values[..., :half_width]
    second_half = values[..., half_width:]
    cos_part = cosine[:, None, :]
    sin_part = sine[:, None, :]
    return jnp.concatenate(
        [
            first_half * cos_part - second_half * sin_part,
            second_half * cos_part + first_half * sin_part,
        ],
        axis=-1,
    )


def attend(query_rows, query_index, keys, key_count):
    scale = 1.0 / math.sqrt(NOPE + ROPE)
    scores = jnp.einsum("rl,kl->rk", query_rows, keys, preferred_element_type=jnp.float32)
    key_index = lax.broadcasted_iota(jnp.int32, (1, key_count), 1)
    visible = key_index <= query_index[:, None]
    scores = jnp.where(visible, scores * scale, masked_value)
    peak = jnp.max(scores, axis=1)
    weights = jnp.where(visible, jnp.exp(scores - peak[:, None]), 0.0)
    totals = jnp.sum(weights, axis=1)
    summed = jnp.dot(
        weights.astype(jnp.bfloat16), keys[:, :LATENT], preferred_element_type=jnp.float32
    )
    return (summed / totals[:, None]).astype(jnp.bfloat16)


def gather_in_order(local, axes):
    acc = local[None]
    for axis, size in axes:
        bit = size // 2
        while bit >= 1:
            upper = (lax.axis_index(axis) // bit) % 2 == 1
            other = lax.ppermute(acc, axis, [(i, i ^ bit) for i in range(size)])
            first = jnp.where(upper, other, acc)
            second = jnp.where(upper, acc, other)
            acc = jnp.stack([first, second], axis=1).reshape((-1,) + local.shape)
            bit //= 2
    return acc.reshape((-1,) + local.shape[1:])


def scatter_sum(partial, axes):
    acc = partial
    for axis, size in axes:
        bit = size // 2
        while bit >= 1:
            upper = (lax.axis_index(axis) // bit) % 2 == 1
            half = acc.shape[1] // 2
            low, high = acc[:, :half], acc[:, half:]
            keep = jnp.where(upper, high, low)
            send = jnp.where(upper, low, high)
            acc = keep + lax.ppermute(send, axis, [(i, i ^ bit) for i in range(size)])
            bit //= 2
    return acc


def upward(latent_out, value_up, token_count, head_count):
    head_out = jnp.einsum(
        "thl,lhd->thd",
        latent_out.reshape(token_count, head_count, LATENT),
        value_up.reshape(LATENT, head_count, VDIM),
        preferred_element_type=jnp.float32,
    )
    return head_out.astype(jnp.bfloat16).reshape(token_count, head_count * VDIM)


def body(queries_nope, queries_rope, latents, rope_keys, positions, key_up, value_up, out_proj):
    token_count = latents.shape[0]
    head_count = key_up.shape[1] // NOPE
    ctx_count = lax.axis_size(CTX)
    cosine, sine = rope_tables(positions, ROPE)
    rot_queries = rotate(
        queries_rope.astype(jnp.float32).reshape(token_count, head_count, ROPE), cosine, sine
    ).astype(jnp.bfloat16)
    rot_keys = rotate(rope_keys.astype(jnp.float32)[:, None, :], cosine, sine)[:, 0, :].astype(
        jnp.bfloat16
    )
    lat_queries = jnp.einsum(
        "thn,lhn->thl",
        queries_nope.reshape(token_count, head_count, NOPE),
        key_up.reshape(LATENT, head_count, NOPE),
        preferred_element_type=jnp.float32,
    ).astype(jnp.bfloat16)
    query_rows = jnp.concatenate([lat_queries, rot_queries], axis=-1).reshape(
        token_count * head_count, LATENT + ROPE
    )
    local_keys = jnp.concatenate([latents, rot_keys], axis=-1)
    keys = gather_in_order(local_keys, CTX_SPLIT)
    first_token = lax.axis_index(CTX) * token_count
    query_index = jnp.repeat(
        first_token + jnp.arange(token_count, dtype=jnp.int32), head_count
    )
    latent_out = attend(query_rows, query_index, keys, token_count * ctx_count)
    head_out = upward(latent_out, value_up, token_count, head_count)
    partial_sums = jnp.dot(
        head_out,
        lax.all_gather(out_proj, CTX, axis=1, tiled=True),
        preferred_element_type=jnp.float32,
    )
    return scatter_sum(partial_sums, HEAD_SPLIT).astype(jnp.bfloat16)


CTX_SPLIT = (("zh", 8), ("zl", 2), ("yl", 2), ("co", 2))
HEAD_SPLIT = (("x", 4), ("yh", 2))
CTX = tuple(name for name, _ in CTX_SPLIT)
HEAD = tuple(name for name, _ in HEAD_SPLIT)


def solution(mesh):
    sizes = tuple(size for _, size in CTX_SPLIT + HEAD_SPLIT)
    fine = Mesh(mesh.devices.reshape(sizes), CTX + HEAD)
    in_specs = (
        P(CTX, HEAD),
        P(CTX, HEAD),
        P(CTX, None),
        P(CTX, None),
        P(CTX),
        P(None, HEAD),
        P(None, HEAD),
        P(HEAD, CTX),
    )
    out_specs = P(CTX, HEAD)
    return jax.shard_map(body, mesh=fine, in_specs=in_specs, out_specs=out_specs, check_vma=False)
```

```python
import math

import jax
import jax.numpy as jnp
from jax import lax
from jax.sharding import Mesh
from jax.sharding import PartitionSpec as P

LATENT = 512
ROPE = 64
NOPE = 128
VDIM = 128


masked_value = -1e30


def rope_tables(token_pos, width):
    half_width = width // 2
    freqs = jnp.exp(jnp.arange(half_width, dtype=jnp.float32) * (-2.0 * math.log(10000.0) / width))
    angle = token_pos.astype(jnp.float32)[:, None] * freqs[None, :]
    return (jnp.cos(angle), jnp.sin(angle))


def rotate(values, cosine, sine):
    half_width = values.shape[-1] // 2
    first_half = values[..., :half_width]
    second_half = values[..., half_width:]
    cos_part = cosine[:, None, :]
    sin_part = sine[:, None, :]
    return jnp.concatenate(
        [
            first_half * cos_part - second_half * sin_part,
            second_half * cos_part + first_half * sin_part,
        ],
        axis=-1,
    )


def attend(query_rows, query_index, keys, key_count):
    scale = 1.0 / math.sqrt(NOPE + ROPE)
    scores = jnp.einsum("rl,kl->rk", query_rows, keys, preferred_element_type=jnp.float32)
    key_index = lax.broadcasted_iota(jnp.int32, (1, key_count), 1)
    visible = key_index <= query_index[:, None]
    scores = jnp.where(visible, scores * scale, masked_value)
    peak = jnp.max(scores, axis=1)
    weights = jnp.where(visible, jnp.exp(scores - peak[:, None]), 0.0)
    totals = jnp.sum(weights, axis=1)
    summed = jnp.dot(
        weights.astype(jnp.bfloat16), keys[:, :LATENT], preferred_element_type=jnp.float32
    )
    return (summed / totals[:, None]).astype(jnp.bfloat16)


def exchange(acc, axis, size, bit, same_over_yh):
    pairs = [(i, i ^ bit) for i in range(size)]
    if axis != "yl" or not same_over_yh:
        return lax.ppermute(acc, axis, pairs)
    half = acc.shape[0] // 2
    near = lax.ppermute(acc[:half], "yl", pairs)
    far = lax.ppermute(acc[half:], ("yl", "yh"), [(i, i ^ 3) for i in range(4)])
    return jnp.concatenate([near, far], axis=0)


def gather_in_order(local, axes, same_over_yh):
    acc = local[None]
    for axis, size in axes:
        bit = size // 2
        while bit >= 1:
            upper = (lax.axis_index(axis) // bit) % 2 == 1
            other = exchange(acc, axis, size, bit, same_over_yh)
            first = jnp.where(upper, other, acc)
            second = jnp.where(upper, acc, other)
            acc = jnp.stack([first, second], axis=1).reshape((-1,) + local.shape)
            bit //= 2
    return acc.reshape((-1,) + local.shape[1:])


def scatter_sum(partial, axes):
    acc = partial
    for axis, size in axes:
        bit = size // 2
        while bit >= 1:
            upper = (lax.axis_index(axis) // bit) % 2 == 1
            half = acc.shape[1] // 2
            low, high = acc[:, :half], acc[:, half:]
            keep = jnp.where(upper, high, low)
            send = jnp.where(upper, low, high)
            acc = keep + lax.ppermute(send, axis, [(i, i ^ bit) for i in range(size)])
            bit //= 2
    return acc


def chip_pair_columns(out_proj):
    blocks = gather_in_order(out_proj.T, (("yl", 2), ("co", 2)), False)
    return blocks.reshape(-1, out_proj.shape[1], out_proj.shape[0]).transpose(2, 0, 1).reshape(
        out_proj.shape[0], -1
    )


def upward(latent_out, value_up, token_count, head_count):
    head_out = jnp.einsum(
        "thl,lhd->thd",
        latent_out.reshape(token_count, head_count, LATENT),
        value_up.reshape(LATENT, head_count, VDIM),
        preferred_element_type=jnp.float32,
    )
    return head_out.astype(jnp.bfloat16).reshape(token_count, head_count * VDIM)


def body(queries_nope, queries_rope, latents, rope_keys, positions, key_up, value_up, out_proj):
    token_count = latents.shape[0]
    head_count = key_up.shape[1] // NOPE
    ctx_count = lax.axis_size(CTX)
    cosine, sine = rope_tables(positions, ROPE)
    rot_queries = rotate(
        queries_rope.astype(jnp.float32).reshape(token_count, head_count, ROPE), cosine, sine
    ).astype(jnp.bfloat16)
    rot_keys = rotate(rope_keys.astype(jnp.float32)[:, None, :], cosine, sine)[:, 0, :].astype(
        jnp.bfloat16
    )
    lat_queries = jnp.einsum(
        "thn,lhn->thl",
        queries_nope.reshape(token_count, head_count, NOPE),
        key_up.reshape(LATENT, head_count, NOPE),
        preferred_element_type=jnp.float32,
    ).astype(jnp.bfloat16)
    query_rows = jnp.concatenate([lat_queries, rot_queries], axis=-1).reshape(
        token_count * head_count, LATENT + ROPE
    )
    local_keys = jnp.concatenate([latents, rot_keys], axis=-1)
    keys = gather_in_order(local_keys, CTX_SPLIT, True)
    first_token = lax.axis_index(CTX) * token_count
    query_index = jnp.repeat(
        first_token + jnp.arange(token_count, dtype=jnp.int32), head_count
    )
    latent_out = attend(query_rows, query_index, keys, token_count * ctx_count)
    head_out = upward(latent_out, value_up, token_count, head_count)
    partial_sums = jnp.dot(
        head_out,
        lax.all_gather(chip_pair_columns(out_proj), ("zh", "zl"), axis=1, tiled=True),
        preferred_element_type=jnp.float32,
    )
    return scatter_sum(partial_sums, HEAD_SPLIT).astype(jnp.bfloat16)


CTX_SPLIT = (("zh", 8), ("zl", 2), ("yl", 2), ("co", 2))
HEAD_SPLIT = (("x", 4), ("yh", 2))
CTX = tuple(name for name, _ in CTX_SPLIT)
HEAD = tuple(name for name, _ in HEAD_SPLIT)


def solution(mesh):
    sizes = tuple(size for _, size in CTX_SPLIT + HEAD_SPLIT)
    fine = Mesh(mesh.devices.reshape(sizes), CTX + HEAD)
    in_specs = (
        P(CTX, HEAD),
        P(CTX, HEAD),
        P(CTX, None),
        P(CTX, None),
        P(CTX),
        P(None, HEAD),
        P(None, HEAD),
        P(HEAD, CTX),
    )
    out_specs = P(CTX, HEAD)
    return jax.shard_map(body, mesh=fine, in_specs=in_specs, out_specs=out_specs, check_vma=False)
```

```python
import math

import jax
import jax.numpy as jnp
from jax import lax
from jax.sharding import Mesh
from jax.sharding import PartitionSpec as P

LATENT = 512
ROPE = 64
NOPE = 128
VDIM = 128


masked_value = -1e30


def rope_tables(token_pos, width):
    half_width = width // 2
    freqs = jnp.exp(jnp.arange(half_width, dtype=jnp.float32) * (-2.0 * math.log(10000.0) / width))
    angle = token_pos.astype(jnp.float32)[:, None] * freqs[None, :]
    return (jnp.cos(angle), jnp.sin(angle))


def rotate(values, cosine, sine):
    half_width = values.shape[-1] // 2
    first_half = values[..., :half_width]
    second_half = values[..., half_width:]
    cos_part = cosine[:, None, :]
    sin_part = sine[:, None, :]
    return jnp.concatenate(
        [
            first_half * cos_part - second_half * sin_part,
            second_half * cos_part + first_half * sin_part,
        ],
        axis=-1,
    )


def attend(query_rows, query_index, keys, key_count):
    scale = 1.0 / math.sqrt(NOPE + ROPE)
    scores = jnp.einsum("rl,kl->rk", query_rows, keys, preferred_element_type=jnp.float32)
    key_index = lax.broadcasted_iota(jnp.int32, (1, key_count), 1)
    visible = key_index <= query_index[:, None]
    scores = jnp.where(visible, scores * scale, masked_value)
    peak = jnp.max(scores, axis=1)
    weights = jnp.where(visible, jnp.exp(scores - peak[:, None]), 0.0)
    totals = jnp.sum(weights, axis=1)
    summed = jnp.dot(
        weights.astype(jnp.bfloat16), keys[:, :LATENT], preferred_element_type=jnp.float32
    )
    return (summed / totals[:, None]).astype(jnp.bfloat16)


def exchange(acc, axis, size, bit, same_over_yh):
    pairs = [(i, i ^ bit) for i in range(size)]
    if axis != "yl" or not same_over_yh:
        return lax.ppermute(acc, axis, pairs)
    half = acc.shape[0] // 2
    near = lax.ppermute(acc[:half], "yl", pairs)
    far = lax.ppermute(acc[half:], ("yl", "yh"), [(i, i ^ 3) for i in range(4)])
    return jnp.concatenate([near, far], axis=0)


def gather_in_order(local, axes, same_over_yh):
    acc = local[None]
    for axis, size in axes:
        bit = size // 2
        while bit >= 1:
            upper = (lax.axis_index(axis) // bit) % 2 == 1
            other = exchange(acc, axis, size, bit, same_over_yh)
            first = jnp.where(upper, other, acc)
            second = jnp.where(upper, acc, other)
            acc = jnp.stack([first, second], axis=1).reshape((-1,) + local.shape)
            bit //= 2
    return acc.reshape((-1,) + local.shape[1:])


def scatter_sum(partial, axes):
    acc = partial
    for axis, size in axes:
        bit = size // 2
        while bit >= 1:
            upper = (lax.axis_index(axis) // bit) % 2 == 1
            half = acc.shape[1] // 2
            low, high = acc[:, :half], acc[:, half:]
            keep = jnp.where(upper, high, low)
            send = jnp.where(upper, low, high)
            acc = keep + lax.ppermute(send, axis, [(i, i ^ bit) for i in range(size)])
            bit //= 2
    return acc


def chip_pair_columns(out_proj):
    blocks = gather_in_order(out_proj.T, (("yl", 2), ("co", 2)), False)
    return blocks.reshape(-1, out_proj.shape[1], out_proj.shape[0]).transpose(2, 0, 1).reshape(
        out_proj.shape[0], -1
    )


def upward(latent_out, value_up, token_count, head_count):
    head_out = jnp.einsum(
        "thl,lhd->thd",
        latent_out.reshape(token_count, head_count, LATENT),
        value_up.reshape(LATENT, head_count, VDIM),
        preferred_element_type=jnp.float32,
    )
    return head_out.astype(jnp.bfloat16).reshape(token_count, head_count * VDIM)


def body(queries_nope, queries_rope, latents, rope_keys, positions, key_up, value_up, out_proj):
    token_count = latents.shape[0]
    head_count = key_up.shape[1] // NOPE
    ctx_count = lax.axis_size(CTX)
    cosine, sine = rope_tables(positions, ROPE)
    rot_queries = rotate(
        queries_rope.astype(jnp.float32).reshape(token_count, head_count, ROPE), cosine, sine
    ).astype(jnp.bfloat16)
    rot_keys = rotate(rope_keys.astype(jnp.float32)[:, None, :], cosine, sine)[:, 0, :].astype(
        jnp.bfloat16
    )
    lat_queries = jnp.einsum(
        "thn,lhn->thl",
        queries_nope.reshape(token_count, head_count, NOPE),
        key_up.reshape(LATENT, head_count, NOPE),
        preferred_element_type=jnp.float32,
    ).astype(jnp.bfloat16)
    query_rows = jnp.concatenate([lat_queries, rot_queries], axis=-1).reshape(
        token_count * head_count, LATENT + ROPE
    )
    local_keys = jnp.concatenate([latents, rot_keys], axis=-1)
    keys = gather_in_order(local_keys, CTX_SPLIT, True)
    first_token = lax.axis_index(CTX) * token_count
    query_index = jnp.repeat(
        first_token + jnp.arange(token_count, dtype=jnp.int32), head_count
    )
    latent_out = attend(query_rows, query_index, keys, token_count * ctx_count)
    head_out = upward(latent_out, value_up, token_count, head_count)
    own = lax.all_gather(out_proj, ("zh", "zl", "yl"), axis=1, tiled=True)
    swapped = lax.ppermute(own, "co", [(0, 1), (1, 0)])
    upper = lax.axis_index("co") == 1
    halves = [jnp.where(upper, swapped, own), jnp.where(upper, own, swapped)]
    partial_sums = jnp.stack(
        [jnp.dot(head_out, half, preferred_element_type=jnp.float32) for half in halves], axis=1
    )
    width = out_proj.shape[1]
    partial_sums = partial_sums.reshape(token_count, 2, -1, width).transpose(0, 2, 1, 3)
    partial_sums = partial_sums.reshape(token_count, -1)
    return scatter_sum(partial_sums, HEAD_SPLIT).astype(jnp.bfloat16)


CTX_SPLIT = (("zh", 8), ("zl", 2), ("yl", 2), ("co", 2))
HEAD_SPLIT = (("x", 4), ("yh", 2))
CTX = tuple(name for name, _ in CTX_SPLIT)
HEAD = tuple(name for name, _ in HEAD_SPLIT)


def solution(mesh):
    sizes = tuple(size for _, size in CTX_SPLIT + HEAD_SPLIT)
    fine = Mesh(mesh.devices.reshape(sizes), CTX + HEAD)
    in_specs = (
        P(CTX, HEAD),
        P(CTX, HEAD),
        P(CTX, None),
        P(CTX, None),
        P(CTX),
        P(None, HEAD),
        P(None, HEAD),
        P(HEAD, CTX),
    )
    out_specs = P(CTX, HEAD)
    return jax.shard_map(body, mesh=fine, in_specs=in_specs, out_specs=out_specs, check_vma=False)
```

```python
import math

import jax
import jax.numpy as jnp
from jax import lax
from jax.sharding import Mesh
from jax.sharding import PartitionSpec as P

LATENT = 512
ROPE = 64
NOPE = 128
VDIM = 128


masked_value = -1e30


def rope_tables(token_pos, width):
    half_width = width // 2
    freqs = jnp.exp(jnp.arange(half_width, dtype=jnp.float32) * (-2.0 * math.log(10000.0) / width))
    angle = token_pos.astype(jnp.float32)[:, None] * freqs[None, :]
    return (jnp.cos(angle), jnp.sin(angle))


def rotate(values, cosine, sine):
    half_width = values.shape[-1] // 2
    first_half = values[..., :half_width]
    second_half = values[..., half_width:]
    cos_part = cosine[:, None, :]
    sin_part = sine[:, None, :]
    return jnp.concatenate(
        [
            first_half * cos_part - second_half * sin_part,
            second_half * cos_part + first_half * sin_part,
        ],
        axis=-1,
    )


def attend(query_rows, query_index, keys, key_count):
    scale = 1.0 / math.sqrt(NOPE + ROPE)
    scores = jnp.einsum("rl,kl->rk", query_rows, keys, preferred_element_type=jnp.float32)
    key_index = lax.broadcasted_iota(jnp.int32, (1, key_count), 1)
    visible = key_index <= query_index[:, None]
    scores = jnp.where(visible, scores * scale, masked_value)
    peak = jnp.max(scores, axis=1)
    weights = jnp.where(visible, jnp.exp(scores - peak[:, None]), 0.0)
    totals = jnp.sum(weights, axis=1)
    summed = jnp.dot(
        weights.astype(jnp.bfloat16), keys[:, :LATENT], preferred_element_type=jnp.float32
    )
    return (summed / totals[:, None]).astype(jnp.bfloat16)


def exchange(acc, axis, size, bit, same_over_yh):
    pairs = [(i, i ^ bit) for i in range(size)]
    if axis != "yl" or not same_over_yh:
        return lax.ppermute(acc, axis, pairs)
    half = acc.shape[0] // 2
    near = lax.ppermute(acc[:half], "yl", pairs)
    far = lax.ppermute(acc[half:], ("yl", "yh"), [(i, i ^ 3) for i in range(4)])
    return jnp.concatenate([near, far], axis=0)


def gather_in_order(local, axes, same_over_yh):
    acc = local[None]
    for axis, size in axes:
        bit = size // 2
        while bit >= 1:
            upper = (lax.axis_index(axis) // bit) % 2 == 1
            other = exchange(acc, axis, size, bit, same_over_yh)
            first = jnp.where(upper, other, acc)
            second = jnp.where(upper, acc, other)
            acc = jnp.stack([first, second], axis=1).reshape((-1,) + local.shape)
            bit //= 2
    return acc.reshape((-1,) + local.shape[1:])


def scatter_sum(partial, axes):
    acc = partial
    for axis, size in axes:
        bit = size // 2
        while bit >= 1:
            upper = (lax.axis_index(axis) // bit) % 2 == 1
            half = acc.shape[1] // 2
            low, high = acc[:, :half], acc[:, half:]
            keep = jnp.where(upper, high, low)
            send = jnp.where(upper, low, high)
            acc = keep + lax.ppermute(send, axis, [(i, i ^ bit) for i in range(size)])
            bit //= 2
    return acc


def upward(latent_out, value_up, token_count, head_count):
    head_out = jnp.einsum(
        "thl,lhd->thd",
        latent_out.reshape(token_count, head_count, LATENT),
        value_up.reshape(LATENT, head_count, VDIM),
        preferred_element_type=jnp.float32,
    )
    return head_out.astype(jnp.bfloat16).reshape(token_count, head_count * VDIM)


def body(queries_nope, queries_rope, latents, rope_keys, positions, key_up, value_up, out_proj):
    token_count = latents.shape[0]
    head_count = key_up.shape[1] // NOPE
    ctx_count = lax.axis_size(CTX)
    cosine, sine = rope_tables(positions, ROPE)
    rot_queries = rotate(
        queries_rope.astype(jnp.float32).reshape(token_count, head_count, ROPE), cosine, sine
    ).astype(jnp.bfloat16)
    rot_keys = rotate(rope_keys.astype(jnp.float32)[:, None, :], cosine, sine)[:, 0, :].astype(
        jnp.bfloat16
    )
    lat_queries = jnp.einsum(
        "thn,lhn->thl",
        queries_nope.reshape(token_count, head_count, NOPE),
        key_up.reshape(LATENT, head_count, NOPE),
        preferred_element_type=jnp.float32,
    ).astype(jnp.bfloat16)
    query_rows = jnp.concatenate([lat_queries, rot_queries], axis=-1).reshape(
        token_count * head_count, LATENT + ROPE
    )
    local_keys = jnp.concatenate([latents, rot_keys], axis=-1)
    keys = gather_in_order(local_keys, CTX_SPLIT, True)
    first_token = lax.axis_index(CTX) * token_count
    query_index = jnp.repeat(
        first_token + jnp.arange(token_count, dtype=jnp.int32), head_count
    )
    latent_out = attend(query_rows, query_index, keys, token_count * ctx_count)
    head_out = upward(latent_out, value_up, token_count, head_count)
    pair = gather_in_order(out_proj.T, (("yl", 2),), False)
    pair = pair.reshape(2, out_proj.shape[1], -1).transpose(2, 0, 1).reshape(out_proj.shape[0], -1)
    own = lax.all_gather(pair, ("zh", "zl"), axis=1, tiled=True)
    swapped = lax.ppermute(own, "co", [(0, 1), (1, 0)])
    upper = lax.axis_index("co") == 1
    halves = [jnp.where(upper, swapped, own), jnp.where(upper, own, swapped)]
    partial_sums = jnp.stack(
        [jnp.dot(head_out, half, preferred_element_type=jnp.float32) for half in halves], axis=1
    )
    width = out_proj.shape[1]
    partial_sums = partial_sums.reshape(token_count, 2, -1, width).transpose(0, 2, 1, 3)
    partial_sums = partial_sums.reshape(token_count, -1)
    return scatter_sum(partial_sums, HEAD_SPLIT).astype(jnp.bfloat16)


CTX_SPLIT = (("zh", 8), ("zl", 2), ("yl", 2), ("co", 2))
HEAD_SPLIT = (("x", 4), ("yh", 2))
CTX = tuple(name for name, _ in CTX_SPLIT)
HEAD = tuple(name for name, _ in HEAD_SPLIT)


def solution(mesh):
    sizes = tuple(size for _, size in CTX_SPLIT + HEAD_SPLIT)
    fine = Mesh(mesh.devices.reshape(sizes), CTX + HEAD)
    in_specs = (
        P(CTX, HEAD),
        P(CTX, HEAD),
        P(CTX, None),
        P(CTX, None),
        P(CTX),
        P(None, HEAD),
        P(None, HEAD),
        P(HEAD, CTX),
    )
    out_specs = P(CTX, HEAD)
    return jax.shard_map(body, mesh=fine, in_specs=in_specs, out_specs=out_specs, check_vma=False)
```

```python
import math

import jax
import jax.numpy as jnp
from jax import lax
from jax.sharding import Mesh
from jax.sharding import PartitionSpec as P

LATENT = 512
ROPE = 64
NOPE = 128
VDIM = 128


masked_value = -1e30


def rope_tables(token_pos, width):
    half_width = width // 2
    freqs = jnp.exp(jnp.arange(half_width, dtype=jnp.float32) * (-2.0 * math.log(10000.0) / width))
    angle = token_pos.astype(jnp.float32)[:, None] * freqs[None, :]
    return (jnp.cos(angle), jnp.sin(angle))


def rotate(values, cosine, sine):
    half_width = values.shape[-1] // 2
    first_half = values[..., :half_width]
    second_half = values[..., half_width:]
    cos_part = cosine[:, None, :]
    sin_part = sine[:, None, :]
    return jnp.concatenate(
        [
            first_half * cos_part - second_half * sin_part,
            second_half * cos_part + first_half * sin_part,
        ],
        axis=-1,
    )


def attend(query_rows, query_index, keys, key_index):
    scale = 1.0 / math.sqrt(NOPE + ROPE)
    scores = jnp.einsum("rl,kl->rk", query_rows, keys, preferred_element_type=jnp.float32)
    visible = key_index <= query_index[:, None]
    scores = jnp.where(visible, scores * scale, masked_value)
    peak = jnp.max(scores, axis=1)
    weights = jnp.where(visible, jnp.exp(scores - peak[:, None]), 0.0)
    totals = jnp.sum(weights, axis=1)
    summed = jnp.dot(
        weights.astype(jnp.bfloat16), keys[:, :LATENT], preferred_element_type=jnp.float32
    )
    return (summed / totals[:, None]).astype(jnp.bfloat16)


def exchange(acc, axis, size, bit, same_over_yh):
    pairs = [(i, i ^ bit) for i in range(size)]
    if axis != "yl" or not same_over_yh:
        return lax.ppermute(acc, axis, pairs)
    half = acc.shape[0] // 2
    near = lax.ppermute(acc[:half], "yl", pairs)
    far = lax.ppermute(acc[half:], ("yl", "yh"), [(i, i ^ 3) for i in range(4)])
    return jnp.concatenate([near, far], axis=0)


def gather_in_order(local, axes, same_over_yh):
    acc = local[None]
    for axis, size in axes:
        bit = size // 2
        while bit >= 1:
            upper = (lax.axis_index(axis) // bit) % 2 == 1
            other = exchange(acc, axis, size, bit, same_over_yh)
            first = jnp.where(upper, other, acc)
            second = jnp.where(upper, acc, other)
            acc = jnp.stack([first, second], axis=1).reshape((-1,) + local.shape)
            bit //= 2
    return acc.reshape((-1,) + local.shape[1:])


ABSENT = 1 << 20


def gather_earlier_keys(local):
    cubes = lax.axis_size("zh")
    cube = lax.axis_index("zh")
    within = lax.axis_index(("zl", "yl", "co"))
    per_cube = lax.axis_size(("zl", "yl", "co"))
    blocks = [local]
    for shift in range(1, cubes):
        blocks.append(lax.ppermute(local, "zh", [(i, i + shift) for i in range(cubes - shift)]))
    acc = jnp.stack(blocks)
    source = cube - jnp.arange(cubes, dtype=jnp.int32)
    index = jnp.where(source >= 0, source * per_cube + within, ABSENT)
    for axis, size in (("zl", 2), ("yl", 2), ("co", 2)):
        step = per_cube // size
        per_cube = step
        other = exchange(acc, axis, size, 1, True)
        acc = jnp.concatenate([acc, other], axis=0)
        index = jnp.concatenate([index, jnp.where(index < ABSENT, index ^ step, ABSENT)])
    return acc, index


def scatter_sum(blocks):
    groups = lax.axis_size(HEAD)
    me = lax.axis_index(HEAD)
    total = blocks[me]
    for shift in range(1, groups):
        total = total + lax.ppermute(
            blocks[me ^ shift], HEAD, [(i, i ^ shift) for i in range(groups)]
        )
    return total


def upward(latent_out, value_up, token_count, head_count):
    head_out = jnp.einsum(
        "thl,lhd->thd",
        latent_out.reshape(token_count, head_count, LATENT),
        value_up.reshape(LATENT, head_count, VDIM),
        preferred_element_type=jnp.float32,
    )
    return head_out.astype(jnp.bfloat16).reshape(token_count, head_count * VDIM)


def body(queries_nope, queries_rope, latents, rope_keys, positions, key_up, value_up, out_proj):
    token_count = latents.shape[0]
    head_count = key_up.shape[1] // NOPE
    cosine, sine = rope_tables(positions, ROPE)
    rot_queries = rotate(
        queries_rope.astype(jnp.float32).reshape(token_count, head_count, ROPE), cosine, sine
    ).astype(jnp.bfloat16)
    rot_keys = rotate(rope_keys.astype(jnp.float32)[:, None, :], cosine, sine)[:, 0, :].astype(
        jnp.bfloat16
    )
    lat_queries = jnp.einsum(
        "thn,lhn->thl",
        queries_nope.reshape(token_count, head_count, NOPE),
        key_up.reshape(LATENT, head_count, NOPE),
        preferred_element_type=jnp.float32,
    ).astype(jnp.bfloat16)
    query_rows = jnp.concatenate([lat_queries, rot_queries], axis=-1).reshape(
        token_count * head_count, LATENT + ROPE
    )
    local_keys = jnp.concatenate([latents, rot_keys], axis=-1)
    key_blocks, block_index = gather_earlier_keys(local_keys)
    keys = key_blocks.reshape(-1, LATENT + ROPE)
    key_index = (
        block_index[:, None] * token_count + jnp.arange(token_count, dtype=jnp.int32)[None, :]
    ).reshape(1, -1)
    first_token = lax.axis_index(CTX) * token_count
    query_index = jnp.repeat(
        first_token + jnp.arange(token_count, dtype=jnp.int32), head_count
    )
    latent_out = attend(query_rows, query_index, keys, key_index)
    head_out = upward(latent_out, value_up, token_count, head_count)
    pair = gather_in_order(out_proj.T, (("yl", 2),), False)
    pair = pair.reshape(2, out_proj.shape[1], -1).transpose(2, 0, 1).reshape(out_proj.shape[0], -1)
    own = lax.all_gather(pair, ("zh", "zl"), axis=1, tiled=True)
    swapped = lax.ppermute(own, "co", [(0, 1), (1, 0)])
    upper = lax.axis_index("co") == 1
    halves = [jnp.where(upper, swapped, own), jnp.where(upper, own, swapped)]
    groups = lax.axis_size(HEAD)
    partial_sums = jnp.concatenate(
        [
            jnp.dot(head_out, half, preferred_element_type=jnp.float32).reshape(
                token_count, groups, -1
            )
            for half in halves
        ],
        axis=2,
    ).transpose(1, 0, 2)
    mine = scatter_sum(partial_sums)
    width = out_proj.shape[1]
    mine = mine.reshape(token_count, 2, -1, width).transpose(0, 2, 1, 3)
    return mine.reshape(token_count, -1).astype(jnp.bfloat16)


CTX_SPLIT = (("zh", 8), ("zl", 2), ("yl", 2), ("co", 2))
HEAD_SPLIT = (("x", 4), ("yh", 2))
CTX = tuple(name for name, _ in CTX_SPLIT)
HEAD = tuple(name for name, _ in HEAD_SPLIT)


def solution(mesh):
    sizes = tuple(size for _, size in CTX_SPLIT + HEAD_SPLIT)
    fine = Mesh(mesh.devices.reshape(sizes), CTX + HEAD)
    in_specs = (
        P(CTX, HEAD),
        P(CTX, HEAD),
        P(CTX, None),
        P(CTX, None),
        P(CTX),
        P(None, HEAD),
        P(None, HEAD),
        P(HEAD, CTX),
    )
    out_specs = P(CTX, HEAD)
    return jax.shard_map(body, mesh=fine, in_specs=in_specs, out_specs=out_specs, check_vma=False)
```

```python
import math

import jax
import jax.numpy as jnp
from jax import lax
from jax.sharding import Mesh
from jax.sharding import PartitionSpec as P

LATENT = 512
ROPE = 64
NOPE = 128
VDIM = 128


masked_value = -1e30


def rope_tables(token_pos, width):
    half_width = width // 2
    freqs = jnp.exp(jnp.arange(half_width, dtype=jnp.float32) * (-2.0 * math.log(10000.0) / width))
    angle = token_pos.astype(jnp.float32)[:, None] * freqs[None, :]
    return (jnp.cos(angle), jnp.sin(angle))


def rotate(values, cosine, sine):
    half_width = values.shape[-1] // 2
    first_half = values[..., :half_width]
    second_half = values[..., half_width:]
    cos_part = cosine[:, None, :]
    sin_part = sine[:, None, :]
    return jnp.concatenate(
        [
            first_half * cos_part - second_half * sin_part,
            second_half * cos_part + first_half * sin_part,
        ],
        axis=-1,
    )


def attend_part(query_rows, query_index, keys, key_index):
    scale = 1.0 / math.sqrt(NOPE + ROPE)
    scores = jnp.einsum("rl,kl->rk", query_rows, keys, preferred_element_type=jnp.float32)
    visible = key_index <= query_index[:, None]
    scores = jnp.where(visible, scores * scale, masked_value)
    peak = jnp.max(scores, axis=1)
    weights = jnp.where(visible, jnp.exp(scores - peak[:, None]), 0.0)
    totals = jnp.sum(weights, axis=1)
    summed = jnp.dot(
        weights.astype(jnp.bfloat16), keys[:, :LATENT], preferred_element_type=jnp.float32
    )
    return peak, totals, summed


def merge_parts(parts):
    peak = parts[0][0]
    for part in parts[1:]:
        peak = jnp.maximum(peak, part[0])
    totals = 0.0
    summed = 0.0
    for part_peak, part_totals, part_summed in parts:
        factor = jnp.exp(part_peak - peak)
        totals = totals + factor * part_totals
        summed = summed + factor[:, None] * part_summed
    return (summed / totals[:, None]).astype(jnp.bfloat16)


def exchange(acc, axis, size, bit, same_over_yh):
    pairs = [(i, i ^ bit) for i in range(size)]
    if axis != "yl" or not same_over_yh:
        return lax.ppermute(acc, axis, pairs)
    half = acc.shape[0] // 2
    near = lax.ppermute(acc[:half], "yl", pairs)
    far = lax.ppermute(acc[half:], ("yl", "yh"), [(i, i ^ 3) for i in range(4)])
    return jnp.concatenate([near, far], axis=0)


def gather_in_order(local, axes, same_over_yh):
    acc = local[None]
    for axis, size in axes:
        bit = size // 2
        while bit >= 1:
            upper = (lax.axis_index(axis) // bit) % 2 == 1
            other = exchange(acc, axis, size, bit, same_over_yh)
            first = jnp.where(upper, other, acc)
            second = jnp.where(upper, acc, other)
            acc = jnp.stack([first, second], axis=1).reshape((-1,) + local.shape)
            bit //= 2
    return acc.reshape((-1,) + local.shape[1:])


ABSENT = 1 << 20


def gather_earlier_keys(local):
    cubes = lax.axis_size("zh")
    cube = lax.axis_index("zh")
    within = lax.axis_index(("zl", "yl", "co"))
    per_cube = lax.axis_size(("zl", "yl", "co"))
    blocks = [local]
    for shift in range(1, cubes):
        blocks.append(lax.ppermute(local, "zh", [(i, i + shift) for i in range(cubes - shift)]))
    acc = jnp.stack(blocks)
    source = cube - jnp.arange(cubes, dtype=jnp.int32)
    index = jnp.where(source >= 0, source * per_cube + within, ABSENT)
    chunks = [(acc, index)]
    for axis, size in (("zl", 2), ("yl", 2), ("co", 2)):
        step = per_cube // size
        per_cube = step
        other = exchange(acc, axis, size, 1, True)
        other_index = jnp.where(index < ABSENT, index ^ step, ABSENT)
        chunks.append((other, other_index))
        acc = jnp.concatenate([acc, other], axis=0)
        index = jnp.concatenate([index, other_index])
    return chunks


def scatter_sum(blocks):
    groups = lax.axis_size(HEAD)
    me = lax.axis_index(HEAD)
    total = blocks[me]
    for shift in range(1, groups):
        total = total + lax.ppermute(
            blocks[me ^ shift], HEAD, [(i, i ^ shift) for i in range(groups)]
        )
    return total


def upward(latent_out, value_up, token_count, head_count):
    head_out = jnp.einsum(
        "thl,lhd->thd",
        latent_out.reshape(token_count, head_count, LATENT),
        value_up.reshape(LATENT, head_count, VDIM),
        preferred_element_type=jnp.float32,
    )
    return head_out.astype(jnp.bfloat16).reshape(token_count, head_count * VDIM)


def body(queries_nope, queries_rope, latents, rope_keys, positions, key_up, value_up, out_proj):
    token_count = latents.shape[0]
    head_count = key_up.shape[1] // NOPE
    cosine, sine = rope_tables(positions, ROPE)
    rot_queries = rotate(
        queries_rope.astype(jnp.float32).reshape(token_count, head_count, ROPE), cosine, sine
    ).astype(jnp.bfloat16)
    rot_keys = rotate(rope_keys.astype(jnp.float32)[:, None, :], cosine, sine)[:, 0, :].astype(
        jnp.bfloat16
    )
    lat_queries = jnp.einsum(
        "thn,lhn->thl",
        queries_nope.reshape(token_count, head_count, NOPE),
        key_up.reshape(LATENT, head_count, NOPE),
        preferred_element_type=jnp.float32,
    ).astype(jnp.bfloat16)
    query_rows = jnp.concatenate([lat_queries, rot_queries], axis=-1).reshape(
        token_count * head_count, LATENT + ROPE
    )
    local_keys = jnp.concatenate([latents, rot_keys], axis=-1)
    first_token = lax.axis_index(CTX) * token_count
    query_index = jnp.repeat(
        first_token + jnp.arange(token_count, dtype=jnp.int32), head_count
    )
    parts = []
    for key_blocks, block_index in gather_earlier_keys(local_keys):
        keys = key_blocks.reshape(-1, LATENT + ROPE)
        key_index = (
            block_index[:, None] * token_count + jnp.arange(token_count, dtype=jnp.int32)[None, :]
        ).reshape(1, -1)
        parts.append(attend_part(query_rows, query_index, keys, key_index))
    latent_out = merge_parts(parts)
    head_out = upward(latent_out, value_up, token_count, head_count)
    pair = gather_in_order(out_proj.T, (("yl", 2),), False)
    pair = pair.reshape(2, out_proj.shape[1], -1).transpose(2, 0, 1).reshape(out_proj.shape[0], -1)
    own = lax.all_gather(pair, ("zh", "zl"), axis=1, tiled=True)
    swapped = lax.ppermute(own, "co", [(0, 1), (1, 0)])
    upper = lax.axis_index("co") == 1
    halves = [jnp.where(upper, swapped, own), jnp.where(upper, own, swapped)]
    groups = lax.axis_size(HEAD)
    partial_sums = jnp.concatenate(
        [
            jnp.dot(head_out, half, preferred_element_type=jnp.float32).reshape(
                token_count, groups, -1
            )
            for half in halves
        ],
        axis=2,
    ).transpose(1, 0, 2)
    mine = scatter_sum(partial_sums)
    width = out_proj.shape[1]
    mine = mine.reshape(token_count, 2, -1, width).transpose(0, 2, 1, 3)
    return mine.reshape(token_count, -1).astype(jnp.bfloat16)


CTX_SPLIT = (("zh", 8), ("zl", 2), ("yl", 2), ("co", 2))
HEAD_SPLIT = (("x", 4), ("yh", 2))
CTX = tuple(name for name, _ in CTX_SPLIT)
HEAD = tuple(name for name, _ in HEAD_SPLIT)


def solution(mesh):
    sizes = tuple(size for _, size in CTX_SPLIT + HEAD_SPLIT)
    fine = Mesh(mesh.devices.reshape(sizes), CTX + HEAD)
    in_specs = (
        P(CTX, HEAD),
        P(CTX, HEAD),
        P(CTX, None),
        P(CTX, None),
        P(CTX),
        P(None, HEAD),
        P(None, HEAD),
        P(HEAD, CTX),
    )
    out_specs = P(CTX, HEAD)
    return jax.shard_map(body, mesh=fine, in_specs=in_specs, out_specs=out_specs, check_vma=False)
```

```python
import math

import jax
import jax.numpy as jnp
from jax import lax
from jax.sharding import Mesh
from jax.sharding import PartitionSpec as P

LATENT = 512
ROPE = 64
NOPE = 128
VDIM = 128


masked_value = -1e30


def rope_tables(token_pos, width):
    half_width = width // 2
    freqs = jnp.exp(jnp.arange(half_width, dtype=jnp.float32) * (-2.0 * math.log(10000.0) / width))
    angle = token_pos.astype(jnp.float32)[:, None] * freqs[None, :]
    return (jnp.cos(angle), jnp.sin(angle))


def rotate(values, cosine, sine):
    half_width = values.shape[-1] // 2
    first_half = values[..., :half_width]
    second_half = values[..., half_width:]
    cos_part = cosine[:, None, :]
    sin_part = sine[:, None, :]
    return jnp.concatenate(
        [
            first_half * cos_part - second_half * sin_part,
            second_half * cos_part + first_half * sin_part,
        ],
        axis=-1,
    )


def attend(query_rows, query_index, keys, key_index):
    scale = 1.0 / math.sqrt(NOPE + ROPE)
    scores = jnp.einsum("rl,kl->rk", query_rows, keys, preferred_element_type=jnp.float32)
    visible = key_index <= query_index[:, None]
    scores = jnp.where(visible, scores * scale, masked_value)
    peak = jnp.max(scores, axis=1)
    weights = jnp.where(visible, jnp.exp(scores - peak[:, None]), 0.0)
    totals = jnp.sum(weights, axis=1)
    summed = jnp.dot(
        weights.astype(jnp.bfloat16), keys[:, :LATENT], preferred_element_type=jnp.float32
    )
    return (summed / totals[:, None]).astype(jnp.bfloat16)


def exchange(acc, axis, size, bit, same_over_yh):
    pairs = [(i, i ^ bit) for i in range(size)]
    if axis != "yl" or not same_over_yh:
        return lax.ppermute(acc, axis, pairs)
    half = acc.shape[0] // 2
    near = lax.ppermute(acc[:half], "yl", pairs)
    far = lax.ppermute(acc[half:], ("yl", "yh"), [(i, i ^ 3) for i in range(4)])
    return jnp.concatenate([near, far], axis=0)


def gather_in_order(local, axes, same_over_yh):
    acc = local[None]
    for axis, size in axes:
        bit = size // 2
        while bit >= 1:
            upper = (lax.axis_index(axis) // bit) % 2 == 1
            other = exchange(acc, axis, size, bit, same_over_yh)
            first = jnp.where(upper, other, acc)
            second = jnp.where(upper, acc, other)
            acc = jnp.stack([first, second], axis=1).reshape((-1,) + local.shape)
            bit //= 2
    return acc.reshape((-1,) + local.shape[1:])


ABSENT = 1 << 20


def gather_earlier_keys(local):
    cubes = lax.axis_size("zh")
    cube = lax.axis_index("zh")
    within = lax.axis_index(("zl", "yl", "co"))
    per_cube = lax.axis_size(("zl", "yl", "co"))
    blocks = [local]
    for shift in range(1, cubes):
        blocks.append(lax.ppermute(local, "zh", [(i, i + shift) for i in range(cubes - shift)]))
    acc = jnp.stack(blocks)
    source = cube - jnp.arange(cubes, dtype=jnp.int32)
    index = jnp.where(source >= 0, source * per_cube + within, ABSENT)
    for axis, size in (("zl", 2), ("yl", 2), ("co", 2)):
        step = per_cube // size
        per_cube = step
        other = exchange(acc, axis, size, 1, True)
        acc = jnp.concatenate([acc, other], axis=0)
        index = jnp.concatenate([index, jnp.where(index < ABSENT, index ^ step, ABSENT)])
    return acc, index


def scatter_sum(blocks):
    rows = lax.axis_size("yh")
    columns = lax.axis_size("x")
    x = lax.axis_index("x")
    yh = lax.axis_index("yh")
    blocks = blocks.reshape((columns, rows) + blocks.shape[1:])
    row_sums = blocks[x]
    for shift in range(1, columns):
        row_sums = row_sums + lax.ppermute(
            blocks[x ^ shift], "x", [(i, i ^ shift) for i in range(columns)]
        )
    total = row_sums[yh]
    for shift in range(1, rows):
        total = total + lax.ppermute(
            row_sums[yh ^ shift], "yh", [(i, i ^ shift) for i in range(rows)]
        )
    return total


def upward(latent_out, value_up, token_count, head_count):
    head_out = jnp.einsum(
        "thl,lhd->thd",
        latent_out.reshape(token_count, head_count, LATENT),
        value_up.reshape(LATENT, head_count, VDIM),
        preferred_element_type=jnp.float32,
    )
    return head_out.astype(jnp.bfloat16).reshape(token_count, head_count * VDIM)


def body(queries_nope, queries_rope, latents, rope_keys, positions, key_up, value_up, out_proj):
    token_count = latents.shape[0]
    head_count = key_up.shape[1] // NOPE
    cosine, sine = rope_tables(positions, ROPE)
    rot_queries = rotate(
        queries_rope.astype(jnp.float32).reshape(token_count, head_count, ROPE), cosine, sine
    ).astype(jnp.bfloat16)
    rot_keys = rotate(rope_keys.astype(jnp.float32)[:, None, :], cosine, sine)[:, 0, :].astype(
        jnp.bfloat16
    )
    lat_queries = jnp.einsum(
        "thn,lhn->thl",
        queries_nope.reshape(token_count, head_count, NOPE),
        key_up.reshape(LATENT, head_count, NOPE),
        preferred_element_type=jnp.float32,
    ).astype(jnp.bfloat16)
    query_rows = jnp.concatenate([lat_queries, rot_queries], axis=-1).reshape(
        token_count * head_count, LATENT + ROPE
    )
    local_keys = jnp.concatenate([latents, rot_keys], axis=-1)
    key_blocks, block_index = gather_earlier_keys(local_keys)
    keys = key_blocks.reshape(-1, LATENT + ROPE)
    key_index = (
        block_index[:, None] * token_count + jnp.arange(token_count, dtype=jnp.int32)[None, :]
    ).reshape(1, -1)
    first_token = lax.axis_index(CTX) * token_count
    query_index = jnp.repeat(
        first_token + jnp.arange(token_count, dtype=jnp.int32), head_count
    )
    latent_out = attend(query_rows, query_index, keys, key_index)
    head_out = upward(latent_out, value_up, token_count, head_count)
    pair = gather_in_order(out_proj.T, (("yl", 2),), False)
    pair = pair.reshape(2, out_proj.shape[1], -1).transpose(2, 0, 1).reshape(out_proj.shape[0], -1)
    own = lax.all_gather(pair, ("zh", "zl"), axis=1, tiled=True)
    swapped = lax.ppermute(own, "co", [(0, 1), (1, 0)])
    upper = lax.axis_index("co") == 1
    halves = [jnp.where(upper, swapped, own), jnp.where(upper, own, swapped)]
    groups = lax.axis_size(HEAD)
    partial_sums = jnp.concatenate(
        [
            jnp.dot(head_out, half, preferred_element_type=jnp.float32).reshape(
                token_count, groups, -1
            )
            for half in halves
        ],
        axis=2,
    ).transpose(1, 0, 2)
    mine = scatter_sum(partial_sums)
    width = out_proj.shape[1]
    mine = mine.reshape(token_count, 2, -1, width).transpose(0, 2, 1, 3)
    return mine.reshape(token_count, -1).astype(jnp.bfloat16)


CTX_SPLIT = (("zh", 8), ("zl", 2), ("yl", 2), ("co", 2))
HEAD_SPLIT = (("x", 4), ("yh", 2))
CTX = tuple(name for name, _ in CTX_SPLIT)
HEAD = tuple(name for name, _ in HEAD_SPLIT)


def solution(mesh):
    sizes = tuple(size for _, size in CTX_SPLIT + HEAD_SPLIT)
    fine = Mesh(mesh.devices.reshape(sizes), CTX + HEAD)
    in_specs = (
        P(CTX, HEAD),
        P(CTX, HEAD),
        P(CTX, None),
        P(CTX, None),
        P(CTX),
        P(None, HEAD),
        P(None, HEAD),
        P(HEAD, CTX),
    )
    out_specs = P(CTX, HEAD)
    return jax.shard_map(body, mesh=fine, in_specs=in_specs, out_specs=out_specs, check_vma=False)
```

```python
import math

import jax
import jax.numpy as jnp
from jax import lax
from jax.experimental import pallas as pl
from jax.sharding import Mesh
from jax.sharding import PartitionSpec as P

LATENT = 512
ROPE = 64
NOPE = 128
VDIM = 128


masked_value = -1e30


def rope_tables(token_pos, width):
    half_width = width // 2
    freqs = jnp.exp(jnp.arange(half_width, dtype=jnp.float32) * (-2.0 * math.log(10000.0) / width))
    angle = token_pos.astype(jnp.float32)[:, None] * freqs[None, :]
    return (jnp.cos(angle), jnp.sin(angle))


def rotate(values, cosine, sine):
    half_width = values.shape[-1] // 2
    first_half = values[..., :half_width]
    second_half = values[..., half_width:]
    cos_part = cosine[:, None, :]
    sin_part = sine[:, None, :]
    return jnp.concatenate(
        [
            first_half * cos_part - second_half * sin_part,
            second_half * cos_part + first_half * sin_part,
        ],
        axis=-1,
    )


def attention_kernel(q_ref, qi_ref, ka_ref, ia_ref, kb_ref, ib_ref, o_ref):
    scale = 1.0 / math.sqrt(NOPE + ROPE)
    queries = q_ref[...]
    query_index = qi_ref[...]

    def masked_scores(k_ref, i_ref):
        scores = lax.dot_general(
            queries, k_ref[...], (((1,), (1,)), ((), ())), preferred_element_type=jnp.float32
        )
        visible = i_ref[...] <= query_index
        return jnp.where(visible, scores * scale, masked_value), visible

    scores_a, visible_a = masked_scores(ka_ref, ia_ref)
    scores_b, visible_b = masked_scores(kb_ref, ib_ref)
    peak = jnp.maximum(
        jnp.max(scores_a, axis=1, keepdims=True), jnp.max(scores_b, axis=1, keepdims=True)
    )
    weights_a = jnp.where(visible_a, jnp.exp(scores_a - peak), 0.0)
    weights_b = jnp.where(visible_b, jnp.exp(scores_b - peak), 0.0)
    totals = jnp.sum(weights_a, axis=1, keepdims=True) + jnp.sum(weights_b, axis=1, keepdims=True)
    summed = jnp.dot(
        weights_a.astype(jnp.bfloat16), ka_ref[:, :LATENT], preferred_element_type=jnp.float32
    )
    summed = summed + jnp.dot(
        weights_b.astype(jnp.bfloat16), kb_ref[:, :LATENT], preferred_element_type=jnp.float32
    )
    o_ref[...] = (summed / totals).astype(jnp.bfloat16)


def attend(query_rows, query_index, halves):
    rows = query_rows.shape[0]
    operands = [query_rows, query_index.reshape(rows, 1)]
    key_count = 0
    for keys, key_index in halves:
        operands += [keys, key_index]
        key_count += keys.shape[0]
    width = query_rows.shape[1]
    cost = pl.CostEstimate(
        flops=2 * rows * key_count * (width + LATENT),
        transcendentals=rows * key_count,
        bytes_accessed=2 * (rows * width + key_count * width + rows * LATENT),
    )
    return pl.pallas_call(
        attention_kernel,
        out_shape=jax.ShapeDtypeStruct((rows, LATENT), jnp.bfloat16),
        cost_estimate=cost,
    )(*operands)


def exchange(acc, axis, size, bit, same_over_yh):
    pairs = [(i, i ^ bit) for i in range(size)]
    if axis != "yl" or not same_over_yh:
        return lax.ppermute(acc, axis, pairs)
    half = acc.shape[0] // 2
    near = lax.ppermute(acc[:half], "yl", pairs)
    far = lax.ppermute(acc[half:], ("yl", "yh"), [(i, i ^ 3) for i in range(4)])
    return jnp.concatenate([near, far], axis=0)


def gather_in_order(local, axes, same_over_yh):
    acc = local[None]
    for axis, size in axes:
        bit = size // 2
        while bit >= 1:
            upper = (lax.axis_index(axis) // bit) % 2 == 1
            other = exchange(acc, axis, size, bit, same_over_yh)
            first = jnp.where(upper, other, acc)
            second = jnp.where(upper, acc, other)
            acc = jnp.stack([first, second], axis=1).reshape((-1,) + local.shape)
            bit //= 2
    return acc.reshape((-1,) + local.shape[1:])


ABSENT = 1 << 20


def gather_earlier_keys(local):
    cubes = lax.axis_size("zh")
    cube = lax.axis_index("zh")
    within = lax.axis_index(("zl", "yl", "co"))
    per_cube = lax.axis_size(("zl", "yl", "co"))
    blocks = [local]
    for shift in range(1, cubes):
        blocks.append(lax.ppermute(local, "zh", [(i, i + shift) for i in range(cubes - shift)]))
    acc = jnp.stack(blocks)
    source = cube - jnp.arange(cubes, dtype=jnp.int32)
    index = jnp.where(source >= 0, source * per_cube + within, ABSENT)
    rounds = (("zl", 2), ("yl", 2), ("co", 2))
    for number, (axis, size) in enumerate(rounds):
        step = per_cube // size
        per_cube = step
        other = exchange(acc, axis, size, 1, True)
        other_index = jnp.where(index < ABSENT, index ^ step, ABSENT)
        if number == len(rounds) - 1:
            return (acc, index), (other, other_index)
        acc = jnp.concatenate([acc, other], axis=0)
        index = jnp.concatenate([index, other_index])


def scatter_sum(blocks):
    rows = lax.axis_size("yh")
    columns = lax.axis_size("x")
    x = lax.axis_index("x")
    yh = lax.axis_index("yh")
    blocks = blocks.reshape((columns, rows) + blocks.shape[1:])
    row_sums = blocks[x]
    for shift in range(1, columns):
        row_sums = row_sums + lax.ppermute(
            blocks[x ^ shift], "x", [(i, i ^ shift) for i in range(columns)]
        )
    total = row_sums[yh]
    for shift in range(1, rows):
        total = total + lax.ppermute(
            row_sums[yh ^ shift], "yh", [(i, i ^ shift) for i in range(rows)]
        )
    return total


def upward(latent_out, value_up, token_count, head_count):
    head_out = jnp.einsum(
        "thl,lhd->thd",
        latent_out.reshape(token_count, head_count, LATENT),
        value_up.reshape(LATENT, head_count, VDIM),
        preferred_element_type=jnp.float32,
    )
    return head_out.astype(jnp.bfloat16).reshape(token_count, head_count * VDIM)


def body(queries_nope, queries_rope, latents, rope_keys, positions, key_up, value_up, out_proj):
    token_count = latents.shape[0]
    head_count = key_up.shape[1] // NOPE
    cosine, sine = rope_tables(positions, ROPE)
    rot_queries = rotate(
        queries_rope.astype(jnp.float32).reshape(token_count, head_count, ROPE), cosine, sine
    ).astype(jnp.bfloat16)
    rot_keys = rotate(rope_keys.astype(jnp.float32)[:, None, :], cosine, sine)[:, 0, :].astype(
        jnp.bfloat16
    )
    lat_queries = jnp.einsum(
        "thn,lhn->thl",
        queries_nope.reshape(token_count, head_count, NOPE),
        key_up.reshape(LATENT, head_count, NOPE),
        preferred_element_type=jnp.float32,
    ).astype(jnp.bfloat16)
    query_rows = jnp.concatenate([lat_queries, rot_queries], axis=-1).reshape(
        token_count * head_count, LATENT + ROPE
    )
    local_keys = jnp.concatenate([latents, rot_keys], axis=-1)
    halves = []
    for key_blocks, block_index in gather_earlier_keys(local_keys):
        keys = key_blocks.reshape(-1, LATENT + ROPE)
        key_index = (
            block_index[:, None] * token_count + jnp.arange(token_count, dtype=jnp.int32)[None, :]
        ).reshape(1, -1)
        halves.append((keys, key_index))
    first_token = lax.axis_index(CTX) * token_count
    query_index = jnp.repeat(
        first_token + jnp.arange(token_count, dtype=jnp.int32), head_count
    )
    latent_out = attend(query_rows, query_index, halves)
    head_out = upward(latent_out, value_up, token_count, head_count)
    pair = gather_in_order(out_proj.T, (("yl", 2),), False)
    pair = pair.reshape(2, out_proj.shape[1], -1).transpose(2, 0, 1).reshape(out_proj.shape[0], -1)
    own = lax.all_gather(pair, ("zh", "zl"), axis=1, tiled=True)
    swapped = lax.ppermute(own, "co", [(0, 1), (1, 0)])
    upper = lax.axis_index("co") == 1
    halves = [jnp.where(upper, swapped, own), jnp.where(upper, own, swapped)]
    groups = lax.axis_size(HEAD)
    partial_sums = jnp.concatenate(
        [
            jnp.dot(head_out, half, preferred_element_type=jnp.float32).reshape(
                token_count, groups, -1
            )
            for half in halves
        ],
        axis=2,
    ).transpose(1, 0, 2)
    mine = scatter_sum(partial_sums)
    width = out_proj.shape[1]
    mine = mine.reshape(token_count, 2, -1, width).transpose(0, 2, 1, 3)
    return mine.reshape(token_count, -1).astype(jnp.bfloat16)


CTX_SPLIT = (("zh", 8), ("zl", 2), ("yl", 2), ("co", 2))
HEAD_SPLIT = (("x", 4), ("yh", 2))
CTX = tuple(name for name, _ in CTX_SPLIT)
HEAD = tuple(name for name, _ in HEAD_SPLIT)


def solution(mesh):
    sizes = tuple(size for _, size in CTX_SPLIT + HEAD_SPLIT)
    fine = Mesh(mesh.devices.reshape(sizes), CTX + HEAD)
    in_specs = (
        P(CTX, HEAD),
        P(CTX, HEAD),
        P(CTX, None),
        P(CTX, None),
        P(CTX),
        P(None, HEAD),
        P(None, HEAD),
        P(HEAD, CTX),
    )
    out_specs = P(CTX, HEAD)
    return jax.shard_map(body, mesh=fine, in_specs=in_specs, out_specs=out_specs, check_vma=False)
```

```python
import math

import jax
import jax.numpy as jnp
from jax import lax
from jax.experimental import pallas as pl
from jax.sharding import Mesh
from jax.sharding import PartitionSpec as P

LATENT = 512
ROPE = 64
NOPE = 128
VDIM = 128


masked_value = -1e30


def rope_tables(token_pos, width):
    half_width = width // 2
    freqs = jnp.exp(jnp.arange(half_width, dtype=jnp.float32) * (-2.0 * math.log(10000.0) / width))
    angle = token_pos.astype(jnp.float32)[:, None] * freqs[None, :]
    return (jnp.cos(angle), jnp.sin(angle))


def rotate(values, cosine, sine):
    half_width = values.shape[-1] // 2
    first_half = values[..., :half_width]
    second_half = values[..., half_width:]
    cos_part = cosine[:, None, :]
    sin_part = sine[:, None, :]
    return jnp.concatenate(
        [
            first_half * cos_part - second_half * sin_part,
            second_half * cos_part + first_half * sin_part,
        ],
        axis=-1,
    )


def attention_kernel(q_ref, qi_ref, ka_ref, ia_ref, kb_ref, ib_ref, o_ref):
    scale = 1.0 / math.sqrt(NOPE + ROPE)
    queries = q_ref[...]
    query_index = qi_ref[...]

    def masked_scores(k_ref, i_ref):
        scores = lax.dot_general(
            queries, k_ref[...], (((1,), (1,)), ((), ())), preferred_element_type=jnp.float32
        )
        visible = i_ref[...] <= query_index
        return jnp.where(visible, scores * scale, masked_value), visible

    scores_a, visible_a = masked_scores(ka_ref, ia_ref)
    scores_b, visible_b = masked_scores(kb_ref, ib_ref)
    peak = jnp.maximum(
        jnp.max(scores_a, axis=1, keepdims=True), jnp.max(scores_b, axis=1, keepdims=True)
    )
    weights_a = jnp.where(visible_a, jnp.exp(scores_a - peak), 0.0)
    weights_b = jnp.where(visible_b, jnp.exp(scores_b - peak), 0.0)
    totals = jnp.sum(weights_a, axis=1, keepdims=True) + jnp.sum(weights_b, axis=1, keepdims=True)
    summed = jnp.dot(
        weights_a.astype(jnp.bfloat16), ka_ref[:, :LATENT], preferred_element_type=jnp.float32
    )
    summed = summed + jnp.dot(
        weights_b.astype(jnp.bfloat16), kb_ref[:, :LATENT], preferred_element_type=jnp.float32
    )
    o_ref[...] = (summed / totals).astype(jnp.bfloat16)


def attend(query_rows, query_index, halves):
    rows = query_rows.shape[0]
    operands = [query_rows, query_index.reshape(rows, 1)]
    key_count = 0
    for keys, key_index in halves:
        operands += [keys, key_index]
        key_count += keys.shape[0]
    width = query_rows.shape[1]
    cost = pl.CostEstimate(
        flops=2 * rows * key_count * (width + LATENT),
        transcendentals=rows * key_count,
        bytes_accessed=2 * (rows * width + key_count * width + rows * LATENT),
    )
    return pl.pallas_call(
        attention_kernel,
        out_shape=jax.ShapeDtypeStruct((rows, LATENT), jnp.bfloat16),
        cost_estimate=cost,
    )(*operands)


def exchange(acc, axis, size, bit, same_over_yh):
    pairs = [(i, i ^ bit) for i in range(size)]
    if axis != "yl" or not same_over_yh:
        return lax.ppermute(acc, axis, pairs)
    half = acc.shape[0] // 2
    near = lax.ppermute(acc[:half], "yl", pairs)
    far = lax.ppermute(acc[half:], ("yl", "yh"), [(i, i ^ 3) for i in range(4)])
    return jnp.concatenate([near, far], axis=0)


def gather_in_order(local, axes, same_over_yh):
    acc = local[None]
    for axis, size in axes:
        bit = size // 2
        while bit >= 1:
            upper = (lax.axis_index(axis) // bit) % 2 == 1
            other = exchange(acc, axis, size, bit, same_over_yh)
            first = jnp.where(upper, other, acc)
            second = jnp.where(upper, acc, other)
            acc = jnp.stack([first, second], axis=1).reshape((-1,) + local.shape)
            bit //= 2
    return acc.reshape((-1,) + local.shape[1:])


ABSENT = 1 << 20


def gather_earlier_keys(local):
    cubes = lax.axis_size("zh")
    cube = lax.axis_index("zh")
    within = lax.axis_index(("zl", "yl", "co"))
    per_cube = lax.axis_size(("zl", "yl", "co"))
    blocks = [local]
    for shift in range(1, cubes):
        blocks.append(lax.ppermute(local, "zh", [(i, i + shift) for i in range(cubes - shift)]))
    acc = jnp.stack(blocks)
    source = cube - jnp.arange(cubes, dtype=jnp.int32)
    index = jnp.where(source >= 0, source * per_cube + within, ABSENT)
    rounds = (("zl", 2), ("yl", 2), ("co", 2))
    for number, (axis, size) in enumerate(rounds):
        step = per_cube // size
        per_cube = step
        other = exchange(acc, axis, size, 1, True)
        other_index = jnp.where(index < ABSENT, index ^ step, ABSENT)
        if number == len(rounds) - 1:
            return (acc, index), (other, other_index)
        acc = jnp.concatenate([acc, other], axis=0)
        index = jnp.concatenate([index, other_index])


def scatter_sum(blocks):
    rows = lax.axis_size("yh")
    columns = lax.axis_size("x")
    x = lax.axis_index("x")
    yh = lax.axis_index("yh")
    blocks = blocks.reshape((columns, rows) + blocks.shape[1:])
    row_sums = blocks[x]
    for shift in range(1, columns):
        sent = blocks[x ^ shift].astype(jnp.bfloat16)
        row_sums = row_sums + lax.ppermute(
            sent, "x", [(i, i ^ shift) for i in range(columns)]
        ).astype(jnp.float32)
    total = row_sums[yh]
    for shift in range(1, rows):
        sent = row_sums[yh ^ shift].astype(jnp.bfloat16)
        total = total + lax.ppermute(
            sent, "yh", [(i, i ^ shift) for i in range(rows)]
        ).astype(jnp.float32)
    return total


def upward(latent_out, value_up, token_count, head_count):
    head_out = jnp.einsum(
        "thl,lhd->thd",
        latent_out.reshape(token_count, head_count, LATENT),
        value_up.reshape(LATENT, head_count, VDIM),
        preferred_element_type=jnp.float32,
    )
    return head_out.astype(jnp.bfloat16).reshape(token_count, head_count * VDIM)


def body(queries_nope, queries_rope, latents, rope_keys, positions, key_up, value_up, out_proj):
    token_count = latents.shape[0]
    head_count = key_up.shape[1] // NOPE
    cosine, sine = rope_tables(positions, ROPE)
    rot_queries = rotate(
        queries_rope.astype(jnp.float32).reshape(token_count, head_count, ROPE), cosine, sine
    ).astype(jnp.bfloat16)
    rot_keys = rotate(rope_keys.astype(jnp.float32)[:, None, :], cosine, sine)[:, 0, :].astype(
        jnp.bfloat16
    )
    lat_queries = jnp.einsum(
        "thn,lhn->thl",
        queries_nope.reshape(token_count, head_count, NOPE),
        key_up.reshape(LATENT, head_count, NOPE),
        preferred_element_type=jnp.float32,
    ).astype(jnp.bfloat16)
    query_rows = jnp.concatenate([lat_queries, rot_queries], axis=-1).reshape(
        token_count * head_count, LATENT + ROPE
    )
    local_keys = jnp.concatenate([latents, rot_keys], axis=-1)
    halves = []
    for key_blocks, block_index in gather_earlier_keys(local_keys):
        keys = key_blocks.reshape(-1, LATENT + ROPE)
        key_index = (
            block_index[:, None] * token_count + jnp.arange(token_count, dtype=jnp.int32)[None, :]
        ).reshape(1, -1)
        halves.append((keys, key_index))
    first_token = lax.axis_index(CTX) * token_count
    query_index = jnp.repeat(
        first_token + jnp.arange(token_count, dtype=jnp.int32), head_count
    )
    latent_out = attend(query_rows, query_index, halves)
    head_out = upward(latent_out, value_up, token_count, head_count)
    pair = gather_in_order(out_proj.T, (("yl", 2),), False)
    pair = pair.reshape(2, out_proj.shape[1], -1).transpose(2, 0, 1).reshape(out_proj.shape[0], -1)
    own = lax.all_gather(pair, ("zh", "zl"), axis=1, tiled=True)
    swapped = lax.ppermute(own, "co", [(0, 1), (1, 0)])
    upper = lax.axis_index("co") == 1
    groups = lax.axis_size(HEAD)
    from_own = jnp.dot(head_out, own, preferred_element_type=jnp.float32)
    from_swapped = jnp.dot(head_out, swapped, preferred_element_type=jnp.float32)
    halves = [jnp.where(upper, from_swapped, from_own), jnp.where(upper, from_own, from_swapped)]
    partial_sums = jnp.concatenate(
        [half.reshape(token_count, groups, -1) for half in halves], axis=2
    ).transpose(1, 0, 2)
    mine = scatter_sum(partial_sums)
    width = out_proj.shape[1]
    mine = mine.reshape(token_count, 2, -1, width).transpose(0, 2, 1, 3)
    return mine.reshape(token_count, -1).astype(jnp.bfloat16)


CTX_SPLIT = (("zh", 8), ("zl", 2), ("yl", 2), ("co", 2))
HEAD_SPLIT = (("x", 4), ("yh", 2))
CTX = tuple(name for name, _ in CTX_SPLIT)
HEAD = tuple(name for name, _ in HEAD_SPLIT)


def solution(mesh):
    sizes = tuple(size for _, size in CTX_SPLIT + HEAD_SPLIT)
    fine = Mesh(mesh.devices.reshape(sizes), CTX + HEAD)
    in_specs = (
        P(CTX, HEAD),
        P(CTX, HEAD),
        P(CTX, None),
        P(CTX, None),
        P(CTX),
        P(None, HEAD),
        P(None, HEAD),
        P(HEAD, CTX),
    )
    out_specs = P(CTX, HEAD)
    return jax.shard_map(body, mesh=fine, in_specs=in_specs, out_specs=out_specs, check_vma=False)
```

```python
import math

import jax
import jax.numpy as jnp
from jax import lax
from jax.experimental import pallas as pl
from jax.sharding import Mesh
from jax.sharding import PartitionSpec as P

LATENT = 512
ROPE = 64
NOPE = 128
VDIM = 128


masked_value = -1e30


def rope_tables(token_pos, width):
    half_width = width // 2
    freqs = jnp.exp(jnp.arange(half_width, dtype=jnp.float32) * (-2.0 * math.log(10000.0) / width))
    angle = token_pos.astype(jnp.float32)[:, None] * freqs[None, :]
    return (jnp.cos(angle), jnp.sin(angle))


def rotate(values, cosine, sine):
    half_width = values.shape[-1] // 2
    first_half = values[..., :half_width]
    second_half = values[..., half_width:]
    cos_part = cosine[:, None, :]
    sin_part = sine[:, None, :]
    return jnp.concatenate(
        [
            first_half * cos_part - second_half * sin_part,
            second_half * cos_part + first_half * sin_part,
        ],
        axis=-1,
    )


def attention_kernel(q_ref, qi_ref, ka_ref, ia_ref, kb_ref, ib_ref, o_ref):
    scale = 1.0 / math.sqrt(NOPE + ROPE)
    queries = q_ref[...]
    query_index = qi_ref[...]

    def masked_scores(k_ref, i_ref):
        scores = lax.dot_general(
            queries, k_ref[...], (((1,), (1,)), ((), ())), preferred_element_type=jnp.float32
        )
        visible = i_ref[...] <= query_index
        return jnp.where(visible, scores * scale, masked_value), visible

    scores_a, visible_a = masked_scores(ka_ref, ia_ref)
    scores_b, visible_b = masked_scores(kb_ref, ib_ref)
    peak = jnp.maximum(
        jnp.max(scores_a, axis=1, keepdims=True), jnp.max(scores_b, axis=1, keepdims=True)
    )
    weights_a = jnp.where(visible_a, jnp.exp(scores_a - peak), 0.0)
    weights_b = jnp.where(visible_b, jnp.exp(scores_b - peak), 0.0)
    totals = jnp.sum(weights_a, axis=1, keepdims=True) + jnp.sum(weights_b, axis=1, keepdims=True)
    summed = jnp.dot(
        weights_a.astype(jnp.bfloat16), ka_ref[:, :LATENT], preferred_element_type=jnp.float32
    )
    summed = summed + jnp.dot(
        weights_b.astype(jnp.bfloat16), kb_ref[:, :LATENT], preferred_element_type=jnp.float32
    )
    o_ref[...] = (summed / totals).astype(jnp.bfloat16)


def attend(query_rows, query_index, halves):
    rows = query_rows.shape[0]
    operands = [query_rows, query_index.reshape(rows, 1)]
    key_count = 0
    for keys, key_index in halves:
        operands += [keys, key_index]
        key_count += keys.shape[0]
    width = query_rows.shape[1]
    cost = pl.CostEstimate(
        flops=2 * rows * key_count * (width + LATENT),
        transcendentals=rows * key_count,
        bytes_accessed=2 * (rows * width + key_count * width + rows * LATENT),
    )
    return pl.pallas_call(
        attention_kernel,
        out_shape=jax.ShapeDtypeStruct((rows, LATENT), jnp.bfloat16),
        cost_estimate=cost,
    )(*operands)


def exchange(acc, axis, size, bit, same_over_yh):
    pairs = [(i, i ^ bit) for i in range(size)]
    if axis != "yl" or not same_over_yh:
        return lax.ppermute(acc, axis, pairs)
    half = acc.shape[0] // 2
    near = lax.ppermute(acc[:half], "yl", pairs)
    far = lax.ppermute(acc[half:], ("yl", "yh"), [(i, i ^ 3) for i in range(4)])
    return jnp.concatenate([near, far], axis=0)


def gather_in_order(local, axes, same_over_yh):
    acc = local[None]
    for axis, size in axes:
        bit = size // 2
        while bit >= 1:
            upper = (lax.axis_index(axis) // bit) % 2 == 1
            other = exchange(acc, axis, size, bit, same_over_yh)
            first = jnp.where(upper, other, acc)
            second = jnp.where(upper, acc, other)
            acc = jnp.stack([first, second], axis=1).reshape((-1,) + local.shape)
            bit //= 2
    return acc.reshape((-1,) + local.shape[1:])


ABSENT = 1 << 20


def gather_earlier_keys(local):
    cubes = lax.axis_size("zh")
    cube = lax.axis_index("zh")
    within = lax.axis_index(("zl", "yl", "co"))
    per_cube = lax.axis_size(("zl", "yl", "co"))
    blocks = [local]
    for shift in range(1, cubes):
        blocks.append(lax.ppermute(local, "zh", [(i, i + shift) for i in range(cubes - shift)]))
    acc = jnp.stack(blocks)
    source = cube - jnp.arange(cubes, dtype=jnp.int32)
    index = jnp.where(source >= 0, source * per_cube + within, ABSENT)
    rounds = (("zl", 2), ("yl", 2), ("co", 2))
    for number, (axis, size) in enumerate(rounds):
        step = per_cube // size
        per_cube = step
        other = exchange(acc, axis, size, 1, True)
        other_index = jnp.where(index < ABSENT, index ^ step, ABSENT)
        if number == len(rounds) - 1:
            return (acc, index), (other, other_index)
        acc = jnp.concatenate([acc, other], axis=0)
        index = jnp.concatenate([index, other_index])


def scatter_sum(blocks):
    rows = lax.axis_size("yh")
    columns = lax.axis_size("x")
    x = lax.axis_index("x")
    yh = lax.axis_index("yh")
    blocks = blocks.reshape((columns, rows) + blocks.shape[1:])
    row_sums = blocks[x]
    for shift in range(1, columns):
        sent = blocks[x ^ shift].astype(jnp.bfloat16)
        row_sums = row_sums + lax.ppermute(
            sent, "x", [(i, i ^ shift) for i in range(columns)]
        ).astype(jnp.float32)
    total = row_sums[yh]
    for shift in range(1, rows):
        sent = row_sums[yh ^ shift].astype(jnp.bfloat16)
        total = total + lax.ppermute(
            sent, "yh", [(i, i ^ shift) for i in range(rows)]
        ).astype(jnp.float32)
    return total


def upward(latent_out, value_up, token_count, head_count):
    head_out = jnp.einsum(
        "thl,lhd->thd",
        latent_out.reshape(token_count, head_count, LATENT),
        value_up.reshape(LATENT, head_count, VDIM),
        preferred_element_type=jnp.float32,
    )
    return head_out.astype(jnp.bfloat16).reshape(token_count, head_count * VDIM)


def body(queries_nope, queries_rope, latents, rope_keys, positions, key_up, value_up, out_proj):
    token_count = latents.shape[0]
    head_count = key_up.shape[1] // NOPE
    cosine, sine = rope_tables(positions, ROPE)
    rot_queries = rotate(
        queries_rope.astype(jnp.float32).reshape(token_count, head_count, ROPE), cosine, sine
    ).astype(jnp.bfloat16)
    rot_keys = rotate(rope_keys.astype(jnp.float32)[:, None, :], cosine, sine)[:, 0, :].astype(
        jnp.bfloat16
    )
    lat_queries = jnp.einsum(
        "thn,lhn->thl",
        queries_nope.reshape(token_count, head_count, NOPE),
        key_up.reshape(LATENT, head_count, NOPE),
        preferred_element_type=jnp.float32,
    ).astype(jnp.bfloat16)
    query_rows = jnp.concatenate([lat_queries, rot_queries], axis=-1).reshape(
        token_count * head_count, LATENT + ROPE
    )
    local_keys = jnp.concatenate([latents, rot_keys], axis=-1)
    halves = []
    for key_blocks, block_index in gather_earlier_keys(local_keys):
        keys = key_blocks.reshape(-1, LATENT + ROPE)
        key_index = (
            block_index[:, None] * token_count + jnp.arange(token_count, dtype=jnp.int32)[None, :]
        ).reshape(1, -1)
        halves.append((keys, key_index))
    first_token = lax.axis_index(CTX) * token_count
    query_index = jnp.repeat(
        first_token + jnp.arange(token_count, dtype=jnp.int32), head_count
    )
    latent_out = attend(query_rows, query_index, halves)
    head_out = upward(latent_out, value_up, token_count, head_count)
    pair = gather_in_order(out_proj.T, (("yl", 2),), False)
    pair = pair.reshape(2, out_proj.shape[1], -1).transpose(2, 0, 1).reshape(out_proj.shape[0], -1)
    own = lax.all_gather(pair, ("zh", "zl"), axis=1, tiled=True)
    swapped = lax.ppermute(own, "co", [(0, 1), (1, 0)])
    upper = lax.axis_index("co") == 1
    groups = lax.axis_size(HEAD)
    halves = [
        jnp.dot(head_out, half, preferred_element_type=jnp.float32).reshape(token_count, groups, -1)
        for half in (own, swapped)
    ]
    partial_sums = jnp.concatenate(halves, axis=2).transpose(1, 0, 2)
    mine = scatter_sum(partial_sums)
    half_width = mine.shape[1] // 2
    mine = jnp.where(
        upper,
        jnp.concatenate([mine[:, half_width:], mine[:, :half_width]], axis=1),
        mine,
    )
    width = out_proj.shape[1]
    mine = mine.reshape(token_count, 2, -1, width).transpose(0, 2, 1, 3)
    return mine.reshape(token_count, -1).astype(jnp.bfloat16)


CTX_SPLIT = (("zh", 8), ("zl", 2), ("yl", 2), ("co", 2))
HEAD_SPLIT = (("x", 4), ("yh", 2))
CTX = tuple(name for name, _ in CTX_SPLIT)
HEAD = tuple(name for name, _ in HEAD_SPLIT)


def solution(mesh):
    sizes = tuple(size for _, size in CTX_SPLIT + HEAD_SPLIT)
    fine = Mesh(mesh.devices.reshape(sizes), CTX + HEAD)
    in_specs = (
        P(CTX, HEAD),
        P(CTX, HEAD),
        P(CTX, None),
        P(CTX, None),
        P(CTX),
        P(None, HEAD),
        P(None, HEAD),
        P(HEAD, CTX),
    )
    out_specs = P(CTX, HEAD)
    return jax.shard_map(body, mesh=fine, in_specs=in_specs, out_specs=out_specs, check_vma=False)
```

```python
import math

import jax
import jax.numpy as jnp
from jax import lax
from jax.experimental import pallas as pl
from jax.sharding import Mesh
from jax.sharding import PartitionSpec as P

LATENT = 512
ROPE = 64
NOPE = 128
VDIM = 128


masked_value = -1e30


def rope_tables(token_pos, width):
    half_width = width // 2
    freqs = jnp.exp(jnp.arange(half_width, dtype=jnp.float32) * (-2.0 * math.log(10000.0) / width))
    angle = token_pos.astype(jnp.float32)[:, None] * freqs[None, :]
    return (jnp.cos(angle), jnp.sin(angle))


def rotate(values, cosine, sine):
    half_width = values.shape[-1] // 2
    first_half = values[..., :half_width]
    second_half = values[..., half_width:]
    cos_part = cosine[:, None, :]
    sin_part = sine[:, None, :]
    return jnp.concatenate(
        [
            first_half * cos_part - second_half * sin_part,
            second_half * cos_part + first_half * sin_part,
        ],
        axis=-1,
    )


def attention_kernel(q_ref, qi_ref, ka_ref, ia_ref, kb_ref, ib_ref, o_ref):
    scale = 1.0 / math.sqrt(NOPE + ROPE)
    queries = q_ref[...]
    query_index = qi_ref[...]

    def masked_scores(k_ref, i_ref):
        scores = lax.dot_general(
            queries, k_ref[...], (((1,), (1,)), ((), ())), preferred_element_type=jnp.float32
        )
        visible = i_ref[...] <= query_index
        return jnp.where(visible, scores * scale, masked_value), visible

    scores_a, visible_a = masked_scores(ka_ref, ia_ref)
    scores_b, visible_b = masked_scores(kb_ref, ib_ref)
    peak = jnp.maximum(
        jnp.max(scores_a, axis=1, keepdims=True), jnp.max(scores_b, axis=1, keepdims=True)
    )
    weights_a = jnp.where(visible_a, jnp.exp(scores_a - peak), 0.0)
    weights_b = jnp.where(visible_b, jnp.exp(scores_b - peak), 0.0)
    totals = jnp.sum(weights_a, axis=1, keepdims=True) + jnp.sum(weights_b, axis=1, keepdims=True)
    summed = jnp.dot(
        weights_a.astype(jnp.bfloat16), ka_ref[:, :LATENT], preferred_element_type=jnp.float32
    )
    summed = summed + jnp.dot(
        weights_b.astype(jnp.bfloat16), kb_ref[:, :LATENT], preferred_element_type=jnp.float32
    )
    o_ref[...] = (summed / totals).astype(jnp.bfloat16)


def attend(query_rows, query_index, halves):
    rows = query_rows.shape[0]
    operands = [query_rows, query_index.reshape(rows, 1)]
    key_count = 0
    for keys, key_index in halves:
        operands += [keys, key_index]
        key_count += keys.shape[0]
    width = query_rows.shape[1]
    cost = pl.CostEstimate(
        flops=2 * rows * key_count * (width + LATENT),
        transcendentals=rows * key_count,
        bytes_accessed=2 * (rows * width + key_count * width + rows * LATENT),
    )
    return pl.pallas_call(
        attention_kernel,
        out_shape=jax.ShapeDtypeStruct((rows, LATENT), jnp.bfloat16),
        cost_estimate=cost,
    )(*operands)


def exchange(acc, axis, size, bit, same_over_yh):
    pairs = [(i, i ^ bit) for i in range(size)]
    if axis != "yl" or not same_over_yh:
        return lax.ppermute(acc, axis, pairs)
    half = acc.shape[0] // 2
    near = lax.ppermute(acc[:half], "yl", pairs)
    far = lax.ppermute(acc[half:], ("yl", "yh"), [(i, i ^ 3) for i in range(4)])
    return jnp.concatenate([near, far], axis=0)


def gather_in_order(local, axes, same_over_yh):
    acc = local[None]
    for axis, size in axes:
        bit = size // 2
        while bit >= 1:
            upper = (lax.axis_index(axis) // bit) % 2 == 1
            other = exchange(acc, axis, size, bit, same_over_yh)
            first = jnp.where(upper, other, acc)
            second = jnp.where(upper, acc, other)
            acc = jnp.stack([first, second], axis=1).reshape((-1,) + local.shape)
            bit //= 2
    return acc.reshape((-1,) + local.shape[1:])


ABSENT = 1 << 20


def gather_earlier_keys(local):
    cubes = lax.axis_size("zh")
    cube = lax.axis_index("zh")
    within = lax.axis_index(("zl", "yl", "co"))
    per_cube = lax.axis_size(("zl", "yl", "co"))
    blocks = [local]
    for shift in range(1, cubes):
        blocks.append(lax.ppermute(local, "zh", [(i, i + shift) for i in range(cubes - shift)]))
    acc = jnp.stack(blocks)
    source = cube - jnp.arange(cubes, dtype=jnp.int32)
    index = jnp.where(source >= 0, source * per_cube + within, ABSENT)
    rounds = (("zl", 2), ("yl", 2), ("co", 2))
    for number, (axis, size) in enumerate(rounds):
        step = per_cube // size
        per_cube = step
        other = exchange(acc, axis, size, 1, True)
        other_index = jnp.where(index < ABSENT, index ^ step, ABSENT)
        if number == len(rounds) - 1:
            return (acc, index), (other, other_index)
        acc = jnp.concatenate([acc, other], axis=0)
        index = jnp.concatenate([index, other_index])


def scatter_sum(head_blocks):
    rows = lax.axis_size("yh")
    columns = lax.axis_size("x")
    x = lax.axis_index("x")
    yh = lax.axis_index("yh")
    received = []
    for shift in range(1, columns):
        sent = head_blocks((x ^ shift) * rows, rows).astype(jnp.bfloat16)
        received.append(lax.ppermute(sent, "x", [(i, i ^ shift) for i in range(columns)]))
    row_sums = head_blocks(x * rows, rows)
    for part in received:
        row_sums = row_sums + part.astype(jnp.float32)
    total = row_sums[yh]
    for shift in range(1, rows):
        sent = row_sums[yh ^ shift].astype(jnp.bfloat16)
        total = total + lax.ppermute(
            sent, "yh", [(i, i ^ shift) for i in range(rows)]
        ).astype(jnp.float32)
    return total


def upward(latent_out, value_up, token_count, head_count):
    head_out = jnp.einsum(
        "thl,lhd->thd",
        latent_out.reshape(token_count, head_count, LATENT),
        value_up.reshape(LATENT, head_count, VDIM),
        preferred_element_type=jnp.float32,
    )
    return head_out.astype(jnp.bfloat16).reshape(token_count, head_count * VDIM)


def body(queries_nope, queries_rope, latents, rope_keys, positions, key_up, value_up, out_proj):
    token_count = latents.shape[0]
    head_count = key_up.shape[1] // NOPE
    cosine, sine = rope_tables(positions, ROPE)
    rot_queries = rotate(
        queries_rope.astype(jnp.float32).reshape(token_count, head_count, ROPE), cosine, sine
    ).astype(jnp.bfloat16)
    rot_keys = rotate(rope_keys.astype(jnp.float32)[:, None, :], cosine, sine)[:, 0, :].astype(
        jnp.bfloat16
    )
    lat_queries = jnp.einsum(
        "thn,lhn->thl",
        queries_nope.reshape(token_count, head_count, NOPE),
        key_up.reshape(LATENT, head_count, NOPE),
        preferred_element_type=jnp.float32,
    ).astype(jnp.bfloat16)
    query_rows = jnp.concatenate([lat_queries, rot_queries], axis=-1).reshape(
        token_count * head_count, LATENT + ROPE
    )
    local_keys = jnp.concatenate([latents, rot_keys], axis=-1)
    halves = []
    for key_blocks, block_index in gather_earlier_keys(local_keys):
        keys = key_blocks.reshape(-1, LATENT + ROPE)
        key_index = (
            block_index[:, None] * token_count + jnp.arange(token_count, dtype=jnp.int32)[None, :]
        ).reshape(1, -1)
        halves.append((keys, key_index))
    first_token = lax.axis_index(CTX) * token_count
    query_index = jnp.repeat(
        first_token + jnp.arange(token_count, dtype=jnp.int32), head_count
    )
    latent_out = attend(query_rows, query_index, halves)
    head_out = upward(latent_out, value_up, token_count, head_count)
    pair = gather_in_order(out_proj.T, (("yl", 2),), False)
    pair = pair.reshape(2, out_proj.shape[1], -1).transpose(2, 0, 1).reshape(out_proj.shape[0], -1)
    own = lax.all_gather(pair, ("zh", "zl"), axis=1, tiled=True)
    swapped = lax.ppermute(own, "co", [(0, 1), (1, 0)])
    upper = lax.axis_index("co") == 1
    groups = lax.axis_size(HEAD)
    own = own.reshape(own.shape[0], groups, -1)
    swapped = swapped.reshape(swapped.shape[0], groups, -1)

    def head_blocks(first_head, count):
        parts = [
            jnp.einsum(
                "tk,kjc->jtc",
                head_out,
                lax.dynamic_slice_in_dim(half, first_head, count, axis=1),
                preferred_element_type=jnp.float32,
            )
            for half in (own, swapped)
        ]
        return jnp.concatenate(parts, axis=2)

    mine = scatter_sum(head_blocks)
    half_width = mine.shape[1] // 2
    mine = jnp.where(
        upper,
        jnp.concatenate([mine[:, half_width:], mine[:, :half_width]], axis=1),
        mine,
    )
    width = out_proj.shape[1]
    mine = mine.reshape(token_count, 2, -1, width).transpose(0, 2, 1, 3)
    return mine.reshape(token_count, -1).astype(jnp.bfloat16)


CTX_SPLIT = (("zh", 8), ("zl", 2), ("yl", 2), ("co", 2))
HEAD_SPLIT = (("x", 4), ("yh", 2))
CTX = tuple(name for name, _ in CTX_SPLIT)
HEAD = tuple(name for name, _ in HEAD_SPLIT)


def solution(mesh):
    sizes = tuple(size for _, size in CTX_SPLIT + HEAD_SPLIT)
    fine = Mesh(mesh.devices.reshape(sizes), CTX + HEAD)
    in_specs = (
        P(CTX, HEAD),
        P(CTX, HEAD),
        P(CTX, None),
        P(CTX, None),
        P(CTX),
        P(None, HEAD),
        P(None, HEAD),
        P(HEAD, CTX),
    )
    out_specs = P(CTX, HEAD)
    return jax.shard_map(body, mesh=fine, in_specs=in_specs, out_specs=out_specs, check_vma=False)
```

```python
import math

import jax
import jax.numpy as jnp
from jax import lax
from jax.experimental import pallas as pl
from jax.sharding import Mesh
from jax.sharding import PartitionSpec as P

LATENT = 512
ROPE = 64
NOPE = 128
VDIM = 128


masked_value = -1e30


def rope_tables(token_pos, width):
    half_width = width // 2
    freqs = jnp.exp(jnp.arange(half_width, dtype=jnp.float32) * (-2.0 * math.log(10000.0) / width))
    angle = token_pos.astype(jnp.float32)[:, None] * freqs[None, :]
    return (jnp.cos(angle), jnp.sin(angle))


def rotate(values, cosine, sine):
    half_width = values.shape[-1] // 2
    first_half = values[..., :half_width]
    second_half = values[..., half_width:]
    cos_part = cosine[:, None, :]
    sin_part = sine[:, None, :]
    return jnp.concatenate(
        [
            first_half * cos_part - second_half * sin_part,
            second_half * cos_part + first_half * sin_part,
        ],
        axis=-1,
    )


def masked_scores(queries, query_index, k_ref, i_ref):
    scale = 1.0 / math.sqrt(NOPE + ROPE)
    scores = lax.dot_general(
        queries, k_ref[...], (((1,), (1,)), ((), ())), preferred_element_type=jnp.float32
    )
    visible = i_ref[...] <= query_index
    return jnp.where(visible, scores * scale, masked_value), visible


def first_kernel(q_ref, qi_ref, k_ref, i_ref, peak_ref, totals_ref, summed_ref):
    scores, visible = masked_scores(q_ref[...], qi_ref[...], k_ref, i_ref)
    peak = jnp.max(scores, axis=1, keepdims=True)
    weights = jnp.where(visible, jnp.exp(scores - peak), 0.0)
    peak_ref[...] = peak
    totals_ref[...] = jnp.sum(weights, axis=1, keepdims=True)
    summed_ref[...] = jnp.dot(
        weights.astype(jnp.bfloat16), k_ref[:, :LATENT], preferred_element_type=jnp.float32
    )


def second_kernel(q_ref, qi_ref, k_ref, i_ref, pa_ref, ta_ref, sa_ref, o_ref):
    scores, visible = masked_scores(q_ref[...], qi_ref[...], k_ref, i_ref)
    first_peak = pa_ref[...]
    peak = jnp.maximum(first_peak, jnp.max(scores, axis=1, keepdims=True))
    weights = jnp.where(visible, jnp.exp(scores - peak), 0.0)
    factor = jnp.exp(first_peak - peak)
    totals = factor * ta_ref[...] + jnp.sum(weights, axis=1, keepdims=True)
    summed = factor * sa_ref[...] + jnp.dot(
        weights.astype(jnp.bfloat16), k_ref[:, :LATENT], preferred_element_type=jnp.float32
    )
    o_ref[...] = (summed / totals).astype(jnp.bfloat16)


def attend(query_rows, query_index, halves):
    rows, width = query_rows.shape
    query_index = query_index.reshape(rows, 1)
    (keys_a, index_a), (keys_b, index_b) = halves
    f32 = jnp.float32

    def cost(key_count):
        return pl.CostEstimate(
            flops=2 * rows * key_count * (width + LATENT),
            transcendentals=rows * key_count,
            bytes_accessed=2 * (rows * width + key_count * width) + 4 * rows * LATENT,
        )

    pieces = pl.pallas_call(
        first_kernel,
        out_shape=(
            jax.ShapeDtypeStruct((rows, 1), f32),
            jax.ShapeDtypeStruct((rows, 1), f32),
            jax.ShapeDtypeStruct((rows, LATENT), f32),
        ),
        cost_estimate=cost(keys_a.shape[0]),
    )(query_rows, query_index, keys_a, index_a)
    return pl.pallas_call(
        second_kernel,
        out_shape=jax.ShapeDtypeStruct((rows, LATENT), jnp.bfloat16),
        cost_estimate=cost(keys_b.shape[0]),
    )(query_rows, query_index, keys_b, index_b, *pieces)


def exchange(acc, axis, size, bit, same_over_yh):
    pairs = [(i, i ^ bit) for i in range(size)]
    if axis != "yl" or not same_over_yh:
        return lax.ppermute(acc, axis, pairs)
    half = acc.shape[0] // 2
    near = lax.ppermute(acc[:half], "yl", pairs)
    far = lax.ppermute(acc[half:], ("yl", "yh"), [(i, i ^ 3) for i in range(4)])
    return jnp.concatenate([near, far], axis=0)


def gather_in_order(local, axes, same_over_yh):
    acc = local[None]
    for axis, size in axes:
        bit = size // 2
        while bit >= 1:
            upper = (lax.axis_index(axis) // bit) % 2 == 1
            other = exchange(acc, axis, size, bit, same_over_yh)
            first = jnp.where(upper, other, acc)
            second = jnp.where(upper, acc, other)
            acc = jnp.stack([first, second], axis=1).reshape((-1,) + local.shape)
            bit //= 2
    return acc.reshape((-1,) + local.shape[1:])


ABSENT = 1 << 20


def gather_earlier_keys(local):
    cubes = lax.axis_size("zh")
    cube = lax.axis_index("zh")
    within = lax.axis_index(("zl", "yl", "co"))
    per_cube = lax.axis_size(("zl", "yl", "co"))
    blocks = [local]
    for shift in range(1, cubes):
        blocks.append(lax.ppermute(local, "zh", [(i, i + shift) for i in range(cubes - shift)]))
    acc = jnp.stack(blocks)
    source = cube - jnp.arange(cubes, dtype=jnp.int32)
    index = jnp.where(source >= 0, source * per_cube + within, ABSENT)
    rounds = (("zl", 2), ("yl", 2), ("co", 2))
    for number, (axis, size) in enumerate(rounds):
        step = per_cube // size
        per_cube = step
        other = exchange(acc, axis, size, 1, True)
        other_index = jnp.where(index < ABSENT, index ^ step, ABSENT)
        if number == len(rounds) - 1:
            return (acc, index), (other, other_index)
        acc = jnp.concatenate([acc, other], axis=0)
        index = jnp.concatenate([index, other_index])


def scatter_sum(blocks):
    rows = lax.axis_size("yh")
    columns = lax.axis_size("x")
    x = lax.axis_index("x")
    yh = lax.axis_index("yh")
    blocks = blocks.reshape((columns, rows) + blocks.shape[1:])
    row_sums = blocks[x]
    for shift in range(1, columns):
        sent = blocks[x ^ shift].astype(jnp.bfloat16)
        row_sums = row_sums + lax.ppermute(
            sent, "x", [(i, i ^ shift) for i in range(columns)]
        ).astype(jnp.float32)
    total = row_sums[yh]
    for shift in range(1, rows):
        sent = row_sums[yh ^ shift].astype(jnp.bfloat16)
        total = total + lax.ppermute(
            sent, "yh", [(i, i ^ shift) for i in range(rows)]
        ).astype(jnp.float32)
    return total


def upward(latent_out, value_up, token_count, head_count):
    head_out = jnp.einsum(
        "thl,lhd->thd",
        latent_out.reshape(token_count, head_count, LATENT),
        value_up.reshape(LATENT, head_count, VDIM),
        preferred_element_type=jnp.float32,
    )
    return head_out.astype(jnp.bfloat16).reshape(token_count, head_count * VDIM)


def body(queries_nope, queries_rope, latents, rope_keys, positions, key_up, value_up, out_proj):
    token_count = latents.shape[0]
    head_count = key_up.shape[1] // NOPE
    cosine, sine = rope_tables(positions, ROPE)
    rot_queries = rotate(
        queries_rope.astype(jnp.float32).reshape(token_count, head_count, ROPE), cosine, sine
    ).astype(jnp.bfloat16)
    rot_keys = rotate(rope_keys.astype(jnp.float32)[:, None, :], cosine, sine)[:, 0, :].astype(
        jnp.bfloat16
    )
    lat_queries = jnp.einsum(
        "thn,lhn->thl",
        queries_nope.reshape(token_count, head_count, NOPE),
        key_up.reshape(LATENT, head_count, NOPE),
        preferred_element_type=jnp.float32,
    ).astype(jnp.bfloat16)
    query_rows = jnp.concatenate([lat_queries, rot_queries], axis=-1).reshape(
        token_count * head_count, LATENT + ROPE
    )
    local_keys = jnp.concatenate([latents, rot_keys], axis=-1)
    halves = []
    for key_blocks, block_index in gather_earlier_keys(local_keys):
        keys = key_blocks.reshape(-1, LATENT + ROPE)
        key_index = (
            block_index[:, None] * token_count + jnp.arange(token_count, dtype=jnp.int32)[None, :]
        ).reshape(1, -1)
        halves.append((keys, key_index))
    first_token = lax.axis_index(CTX) * token_count
    query_index = jnp.repeat(
        first_token + jnp.arange(token_count, dtype=jnp.int32), head_count
    )
    latent_out = attend(query_rows, query_index, halves)
    head_out = upward(latent_out, value_up, token_count, head_count)
    pair = gather_in_order(out_proj.T, (("yl", 2),), False)
    pair = pair.reshape(2, out_proj.shape[1], -1).transpose(2, 0, 1).reshape(out_proj.shape[0], -1)
    own = lax.all_gather(pair, ("zh", "zl"), axis=1, tiled=True)
    swapped = lax.ppermute(own, "co", [(0, 1), (1, 0)])
    upper = lax.axis_index("co") == 1
    groups = lax.axis_size(HEAD)
    halves = [
        jnp.dot(head_out, half, preferred_element_type=jnp.float32).reshape(token_count, groups, -1)
        for half in (own, swapped)
    ]
    partial_sums = jnp.concatenate(halves, axis=2).transpose(1, 0, 2)
    mine = scatter_sum(partial_sums)
    half_width = mine.shape[1] // 2
    mine = jnp.where(
        upper,
        jnp.concatenate([mine[:, half_width:], mine[:, :half_width]], axis=1),
        mine,
    )
    width = out_proj.shape[1]
    mine = mine.reshape(token_count, 2, -1, width).transpose(0, 2, 1, 3)
    return mine.reshape(token_count, -1).astype(jnp.bfloat16)


CTX_SPLIT = (("zh", 8), ("zl", 2), ("yl", 2), ("co", 2))
HEAD_SPLIT = (("x", 4), ("yh", 2))
CTX = tuple(name for name, _ in CTX_SPLIT)
HEAD = tuple(name for name, _ in HEAD_SPLIT)


def solution(mesh):
    sizes = tuple(size for _, size in CTX_SPLIT + HEAD_SPLIT)
    fine = Mesh(mesh.devices.reshape(sizes), CTX + HEAD)
    in_specs = (
        P(CTX, HEAD),
        P(CTX, HEAD),
        P(CTX, None),
        P(CTX, None),
        P(CTX),
        P(None, HEAD),
        P(None, HEAD),
        P(HEAD, CTX),
    )
    out_specs = P(CTX, HEAD)
    return jax.shard_map(body, mesh=fine, in_specs=in_specs, out_specs=out_specs, check_vma=False)
```

```python
import math

import jax
import jax.numpy as jnp
from jax import lax
from jax.experimental import pallas as pl
from jax.sharding import Mesh
from jax.sharding import PartitionSpec as P

LATENT = 512
ROPE = 64
NOPE = 128
VDIM = 128


masked_value = -1e30


def rope_tables(token_pos, width):
    half_width = width // 2
    freqs = jnp.exp(jnp.arange(half_width, dtype=jnp.float32) * (-2.0 * math.log(10000.0) / width))
    angle = token_pos.astype(jnp.float32)[:, None] * freqs[None, :]
    return (jnp.cos(angle), jnp.sin(angle))


def rotate(values, cosine, sine):
    half_width = values.shape[-1] // 2
    first_half = values[..., :half_width]
    second_half = values[..., half_width:]
    cos_part = cosine[:, None, :]
    sin_part = sine[:, None, :]
    return jnp.concatenate(
        [
            first_half * cos_part - second_half * sin_part,
            second_half * cos_part + first_half * sin_part,
        ],
        axis=-1,
    )


def attention_kernel(q_ref, qi_ref, ka_ref, ia_ref, kb_ref, ib_ref, v_ref, o_ref):
    scale = 1.0 / math.sqrt(NOPE + ROPE)
    queries = q_ref[...]
    query_index = qi_ref[...]

    def masked_scores(k_ref, i_ref):
        scores = lax.dot_general(
            queries, k_ref[...], (((1,), (1,)), ((), ())), preferred_element_type=jnp.float32
        )
        visible = i_ref[...] <= query_index
        return jnp.where(visible, scores * scale, masked_value), visible

    scores_a, visible_a = masked_scores(ka_ref, ia_ref)
    scores_b, visible_b = masked_scores(kb_ref, ib_ref)
    peak = jnp.maximum(
        jnp.max(scores_a, axis=1, keepdims=True), jnp.max(scores_b, axis=1, keepdims=True)
    )
    weights_a = jnp.where(visible_a, jnp.exp(scores_a - peak), 0.0)
    weights_b = jnp.where(visible_b, jnp.exp(scores_b - peak), 0.0)
    totals = jnp.sum(weights_a, axis=1, keepdims=True) + jnp.sum(weights_b, axis=1, keepdims=True)
    summed = jnp.dot(
        weights_a.astype(jnp.bfloat16), ka_ref[:, :LATENT], preferred_element_type=jnp.float32
    )
    summed = summed + jnp.dot(
        weights_b.astype(jnp.bfloat16), kb_ref[:, :LATENT], preferred_element_type=jnp.float32
    )
    latent_out = (summed / totals).astype(jnp.bfloat16)
    head_count = v_ref.shape[1] // VDIM
    tokens = latent_out.shape[0] // head_count
    for head in range(head_count):
        head_out = jnp.dot(
            latent_out[head * tokens : (head + 1) * tokens],
            v_ref[:, head * VDIM : (head + 1) * VDIM],
            preferred_element_type=jnp.float32,
        )
        o_ref[:, head * VDIM : (head + 1) * VDIM] = head_out.astype(jnp.bfloat16)


def attend(query_rows, query_index, halves, value_up):
    rows = query_rows.shape[0]
    operands = [query_rows, query_index.reshape(rows, 1)]
    key_count = 0
    for keys, key_index in halves:
        operands += [keys, key_index]
        key_count += keys.shape[0]
    width = query_rows.shape[1]
    cost = pl.CostEstimate(
        flops=2 * rows * key_count * (width + LATENT),
        transcendentals=rows * key_count,
        bytes_accessed=2 * (rows * width + key_count * width + rows * LATENT),
    )
    operands.append(value_up)
    tokens = rows * VDIM // value_up.shape[1]
    return pl.pallas_call(
        attention_kernel,
        out_shape=jax.ShapeDtypeStruct((tokens, value_up.shape[1]), jnp.bfloat16),
        cost_estimate=cost,
    )(*operands)


def exchange(acc, axis, size, bit, same_over_yh):
    pairs = [(i, i ^ bit) for i in range(size)]
    if axis != "yl" or not same_over_yh:
        return lax.ppermute(acc, axis, pairs)
    half = acc.shape[0] // 2
    near = lax.ppermute(acc[:half], "yl", pairs)
    far = lax.ppermute(acc[half:], ("yl", "yh"), [(i, i ^ 3) for i in range(4)])
    return jnp.concatenate([near, far], axis=0)


def gather_in_order(local, axes, same_over_yh):
    acc = local[None]
    for axis, size in axes:
        bit = size // 2
        while bit >= 1:
            upper = (lax.axis_index(axis) // bit) % 2 == 1
            other = exchange(acc, axis, size, bit, same_over_yh)
            first = jnp.where(upper, other, acc)
            second = jnp.where(upper, acc, other)
            acc = jnp.stack([first, second], axis=1).reshape((-1,) + local.shape)
            bit //= 2
    return acc.reshape((-1,) + local.shape[1:])


ABSENT = 1 << 20


def gather_earlier_keys(local):
    cubes = lax.axis_size("zh")
    cube = lax.axis_index("zh")
    within = lax.axis_index(("zl", "yl", "co"))
    per_cube = lax.axis_size(("zl", "yl", "co"))
    blocks = [local]
    for shift in range(1, cubes):
        blocks.append(lax.ppermute(local, "zh", [(i, i + shift) for i in range(cubes - shift)]))
    acc = jnp.stack(blocks)
    source = cube - jnp.arange(cubes, dtype=jnp.int32)
    index = jnp.where(source >= 0, source * per_cube + within, ABSENT)
    rounds = (("zl", 2), ("yl", 2), ("co", 2))
    for number, (axis, size) in enumerate(rounds):
        step = per_cube // size
        per_cube = step
        other = exchange(acc, axis, size, 1, True)
        other_index = jnp.where(index < ABSENT, index ^ step, ABSENT)
        if number == len(rounds) - 1:
            return (acc, index), (other, other_index)
        acc = jnp.concatenate([acc, other], axis=0)
        index = jnp.concatenate([index, other_index])


def scatter_sum(blocks):
    rows = lax.axis_size("yh")
    columns = lax.axis_size("x")
    x = lax.axis_index("x")
    yh = lax.axis_index("yh")
    blocks = blocks.reshape((columns, rows) + blocks.shape[1:])
    row_sums = blocks[x]
    for shift in range(1, columns):
        sent = blocks[x ^ shift].astype(jnp.bfloat16)
        row_sums = row_sums + lax.ppermute(
            sent, "x", [(i, i ^ shift) for i in range(columns)]
        ).astype(jnp.float32)
    total = row_sums[yh]
    for shift in range(1, rows):
        sent = row_sums[yh ^ shift].astype(jnp.bfloat16)
        total = total + lax.ppermute(
            sent, "yh", [(i, i ^ shift) for i in range(rows)]
        ).astype(jnp.float32)
    return total


def body(queries_nope, queries_rope, latents, rope_keys, positions, key_up, value_up, out_proj):
    token_count = latents.shape[0]
    head_count = key_up.shape[1] // NOPE
    cosine, sine = rope_tables(positions, ROPE)
    rot_queries = rotate(
        queries_rope.astype(jnp.float32).reshape(token_count, head_count, ROPE), cosine, sine
    ).astype(jnp.bfloat16)
    rot_keys = rotate(rope_keys.astype(jnp.float32)[:, None, :], cosine, sine)[:, 0, :].astype(
        jnp.bfloat16
    )
    lat_queries = jnp.einsum(
        "thn,lhn->thl",
        queries_nope.reshape(token_count, head_count, NOPE),
        key_up.reshape(LATENT, head_count, NOPE),
        preferred_element_type=jnp.float32,
    ).astype(jnp.bfloat16)
    query_rows = (
        jnp.concatenate([lat_queries, rot_queries], axis=-1)
        .transpose(1, 0, 2)
        .reshape(head_count * token_count, LATENT + ROPE)
    )
    local_keys = jnp.concatenate([latents, rot_keys], axis=-1)
    halves = []
    for key_blocks, block_index in gather_earlier_keys(local_keys):
        keys = key_blocks.reshape(-1, LATENT + ROPE)
        key_index = (
            block_index[:, None] * token_count + jnp.arange(token_count, dtype=jnp.int32)[None, :]
        ).reshape(1, -1)
        halves.append((keys, key_index))
    first_token = lax.axis_index(CTX) * token_count
    query_index = jnp.tile(first_token + jnp.arange(token_count, dtype=jnp.int32), head_count)
    head_out = attend(query_rows, query_index, halves, value_up)
    pair = gather_in_order(out_proj.T, (("yl", 2),), False)
    pair = pair.reshape(2, out_proj.shape[1], -1).transpose(2, 0, 1).reshape(out_proj.shape[0], -1)
    own = lax.all_gather(pair, ("zh", "zl"), axis=1, tiled=True)
    swapped = lax.ppermute(own, "co", [(0, 1), (1, 0)])
    upper = lax.axis_index("co") == 1
    groups = lax.axis_size(HEAD)
    halves = [
        jnp.dot(head_out, half, preferred_element_type=jnp.float32).reshape(token_count, groups, -1)
        for half in (own, swapped)
    ]
    partial_sums = jnp.concatenate(halves, axis=2).transpose(1, 0, 2)
    mine = scatter_sum(partial_sums)
    half_width = mine.shape[1] // 2
    mine = jnp.where(
        upper,
        jnp.concatenate([mine[:, half_width:], mine[:, :half_width]], axis=1),
        mine,
    )
    width = out_proj.shape[1]
    mine = mine.reshape(token_count, 2, -1, width).transpose(0, 2, 1, 3)
    return mine.reshape(token_count, -1).astype(jnp.bfloat16)


CTX_SPLIT = (("zh", 8), ("zl", 2), ("yl", 2), ("co", 2))
HEAD_SPLIT = (("x", 4), ("yh", 2))
CTX = tuple(name for name, _ in CTX_SPLIT)
HEAD = tuple(name for name, _ in HEAD_SPLIT)


def solution(mesh):
    sizes = tuple(size for _, size in CTX_SPLIT + HEAD_SPLIT)
    fine = Mesh(mesh.devices.reshape(sizes), CTX + HEAD)
    in_specs = (
        P(CTX, HEAD),
        P(CTX, HEAD),
        P(CTX, None),
        P(CTX, None),
        P(CTX),
        P(None, HEAD),
        P(None, HEAD),
        P(HEAD, CTX),
    )
    out_specs = P(CTX, HEAD)
    return jax.shard_map(body, mesh=fine, in_specs=in_specs, out_specs=out_specs, check_vma=False)
```

```python
import math

import jax
import jax.numpy as jnp
from jax import lax
from jax.experimental import pallas as pl
from jax.sharding import Mesh
from jax.sharding import PartitionSpec as P

LATENT = 512
ROPE = 64
NOPE = 128
VDIM = 128


masked_value = -1e30


def rope_tables(token_pos, width):
    half_width = width // 2
    freqs = jnp.exp(jnp.arange(half_width, dtype=jnp.float32) * (-2.0 * math.log(10000.0) / width))
    angle = token_pos.astype(jnp.float32)[:, None] * freqs[None, :]
    return (jnp.cos(angle), jnp.sin(angle))


def rotate(values, cosine, sine):
    half_width = values.shape[-1] // 2
    first_half = values[..., :half_width]
    second_half = values[..., half_width:]
    cos_part = cosine[:, None, :]
    sin_part = sine[:, None, :]
    return jnp.concatenate(
        [
            first_half * cos_part - second_half * sin_part,
            second_half * cos_part + first_half * sin_part,
        ],
        axis=-1,
    )


def attention_kernel(q_ref, qi_ref, ka_ref, ia_ref, kb_ref, ib_ref, v_ref, o_ref):
    scale = 1.0 / math.sqrt(NOPE + ROPE)
    queries = q_ref[...]
    query_index = qi_ref[...]

    def masked_scores(k_ref, i_ref):
        scores = lax.dot_general(
            queries, k_ref[...], (((1,), (1,)), ((), ())), preferred_element_type=jnp.float32
        )
        visible = i_ref[...] <= query_index
        return jnp.where(visible, scores * scale, masked_value), visible

    scores_a, visible_a = masked_scores(ka_ref, ia_ref)
    scores_b, visible_b = masked_scores(kb_ref, ib_ref)
    peak = jnp.maximum(
        jnp.max(scores_a, axis=1, keepdims=True), jnp.max(scores_b, axis=1, keepdims=True)
    )
    weights_a = jnp.where(visible_a, jnp.exp(scores_a - peak), 0.0)
    weights_b = jnp.where(visible_b, jnp.exp(scores_b - peak), 0.0)
    totals = jnp.sum(weights_a, axis=1, keepdims=True) + jnp.sum(weights_b, axis=1, keepdims=True)
    summed = jnp.dot(
        weights_a.astype(jnp.bfloat16), ka_ref[:, :LATENT], preferred_element_type=jnp.float32
    )
    summed = summed + jnp.dot(
        weights_b.astype(jnp.bfloat16), kb_ref[:, :LATENT], preferred_element_type=jnp.float32
    )
    latent_out = (summed / totals).astype(jnp.bfloat16)
    head_count = v_ref.shape[1] // VDIM
    tokens = latent_out.shape[0] // head_count
    for head in range(head_count):
        head_out = jnp.dot(
            latent_out[head * tokens : (head + 1) * tokens],
            v_ref[:, head * VDIM : (head + 1) * VDIM],
            preferred_element_type=jnp.float32,
        )
        o_ref[:, head * VDIM : (head + 1) * VDIM] = head_out.astype(jnp.bfloat16)


def attend(query_rows, query_index, halves, value_up):
    rows = query_rows.shape[0]
    operands = [query_rows, query_index.reshape(rows, 1)]
    key_count = 0
    for keys, key_index in halves:
        operands += [keys, key_index]
        key_count += keys.shape[0]
    width = query_rows.shape[1]
    cost = pl.CostEstimate(
        flops=2 * rows * key_count * (width + LATENT),
        transcendentals=rows * key_count,
        bytes_accessed=2 * (rows * width + key_count * width + rows * LATENT),
    )
    operands.append(value_up)
    tokens = rows * VDIM // value_up.shape[1]
    return pl.pallas_call(
        attention_kernel,
        out_shape=jax.ShapeDtypeStruct((tokens, value_up.shape[1]), jnp.bfloat16),
        cost_estimate=cost,
    )(*operands)


def exchange(acc, axis, size, bit, same_over_yh):
    pairs = [(i, i ^ bit) for i in range(size)]
    if axis != "yl" or not same_over_yh:
        return lax.ppermute(acc, axis, pairs)
    half = acc.shape[0] // 2
    near = lax.ppermute(acc[:half], "yl", pairs)
    far = lax.ppermute(acc[half:], ("yl", "yh"), [(i, i ^ 3) for i in range(4)])
    return jnp.concatenate([near, far], axis=0)


def gather_in_order(local, axes, same_over_yh):
    acc = local[None]
    for axis, size in axes:
        bit = size // 2
        while bit >= 1:
            upper = (lax.axis_index(axis) // bit) % 2 == 1
            other = exchange(acc, axis, size, bit, same_over_yh)
            first = jnp.where(upper, other, acc)
            second = jnp.where(upper, acc, other)
            acc = jnp.stack([first, second], axis=1).reshape((-1,) + local.shape)
            bit //= 2
    return acc.reshape((-1,) + local.shape[1:])


ABSENT = 1 << 20


def gather_earlier_keys(local):
    cubes = lax.axis_size("zh")
    cube = lax.axis_index("zh")
    within = lax.axis_index(("zl", "yl", "co"))
    per_cube = lax.axis_size(("zl", "yl", "co"))
    blocks = [local]
    for shift in range(1, cubes):
        blocks.append(lax.ppermute(local, "zh", [(i, i + shift) for i in range(cubes - shift)]))
    acc = jnp.stack(blocks)
    source = cube - jnp.arange(cubes, dtype=jnp.int32)
    index = jnp.where(source >= 0, source * per_cube + within, ABSENT)
    rounds = (("zl", 2), ("yl", 2), ("co", 2))
    for number, (axis, size) in enumerate(rounds):
        step = per_cube // size
        per_cube = step
        other = exchange(acc, axis, size, 1, True)
        other_index = jnp.where(index < ABSENT, index ^ step, ABSENT)
        if number == len(rounds) - 1:
            return (acc, index), (other, other_index)
        acc = jnp.concatenate([acc, other], axis=0)
        index = jnp.concatenate([index, other_index])


def scatter_sum(blocks):
    rows = lax.axis_size("yh")
    columns = lax.axis_size("x")
    x = lax.axis_index("x")
    yh = lax.axis_index("yh")
    blocks = blocks.reshape((columns, rows) + blocks.shape[1:])
    row_sums = blocks[x]
    for shift in range(1, columns):
        sent = blocks[x ^ shift].astype(jnp.bfloat16)
        row_sums = row_sums + lax.ppermute(
            sent, "x", [(i, i ^ shift) for i in range(columns)]
        ).astype(jnp.float32)
    total = row_sums[yh]
    for shift in range(1, rows):
        sent = row_sums[yh ^ shift].astype(jnp.bfloat16)
        total = total + lax.ppermute(
            sent, "yh", [(i, i ^ shift) for i in range(rows)]
        ).astype(jnp.float32)
    return total


def body(queries_nope, queries_rope, latents, rope_keys, positions, key_up, value_up, out_proj):
    token_count = latents.shape[0]
    head_count = key_up.shape[1] // NOPE
    cosine, sine = rope_tables(positions, ROPE)
    rot_queries = rotate(
        queries_rope.astype(jnp.float32).reshape(token_count, head_count, ROPE), cosine, sine
    ).astype(jnp.bfloat16)
    rot_keys = rotate(rope_keys.astype(jnp.float32)[:, None, :], cosine, sine)[:, 0, :].astype(
        jnp.bfloat16
    )
    lat_queries = jnp.einsum(
        "thn,lhn->thl",
        queries_nope.reshape(token_count, head_count, NOPE),
        key_up.reshape(LATENT, head_count, NOPE),
        preferred_element_type=jnp.float32,
    ).astype(jnp.bfloat16)
    query_rows = (
        jnp.concatenate([lat_queries, rot_queries], axis=-1)
        .transpose(1, 0, 2)
        .reshape(head_count * token_count, LATENT + ROPE)
    )
    local_keys = jnp.concatenate([latents, rot_keys], axis=-1)
    halves = []
    for key_blocks, block_index in gather_earlier_keys(local_keys):
        keys = key_blocks.reshape(-1, LATENT + ROPE)
        key_index = (
            block_index[:, None] * token_count + jnp.arange(token_count, dtype=jnp.int32)[None, :]
        ).reshape(1, -1)
        halves.append((keys, key_index))
    first_token = lax.axis_index(CTX) * token_count
    query_index = jnp.tile(first_token + jnp.arange(token_count, dtype=jnp.int32), head_count)
    head_out = attend(query_rows, query_index, halves, value_up)
    partner = lax.ppermute(out_proj, "yl", [(0, 1), (1, 0)])
    pair = jnp.concatenate([out_proj, partner], axis=1)
    own = lax.all_gather(pair, ("zh", "zl"), axis=1, tiled=True)
    swapped = lax.ppermute(own, "co", [(0, 1), (1, 0)])
    upper = lax.axis_index("co") == 1
    groups = lax.axis_size(HEAD)
    halves = [
        jnp.dot(head_out, half, preferred_element_type=jnp.float32).reshape(token_count, groups, -1)
        for half in (own, swapped)
    ]
    partial_sums = jnp.concatenate(halves, axis=2).transpose(1, 0, 2)
    mine = scatter_sum(partial_sums)
    half_width = mine.shape[1] // 2
    mine = jnp.where(
        upper,
        jnp.concatenate([mine[:, half_width:], mine[:, :half_width]], axis=1),
        mine,
    )
    width = out_proj.shape[1]
    mine = mine.reshape(token_count, 2, -1, 2, width)
    mine = jnp.where(lax.axis_index("yl") == 1, mine[:, :, :, ::-1, :], mine)
    mine = mine.transpose(0, 2, 3, 1, 4)
    return mine.reshape(token_count, -1).astype(jnp.bfloat16)


CTX_SPLIT = (("zh", 8), ("zl", 2), ("yl", 2), ("co", 2))
HEAD_SPLIT = (("x", 4), ("yh", 2))
CTX = tuple(name for name, _ in CTX_SPLIT)
HEAD = tuple(name for name, _ in HEAD_SPLIT)


def solution(mesh):
    sizes = tuple(size for _, size in CTX_SPLIT + HEAD_SPLIT)
    fine = Mesh(mesh.devices.reshape(sizes), CTX + HEAD)
    in_specs = (
        P(CTX, HEAD),
        P(CTX, HEAD),
        P(CTX, None),
        P(CTX, None),
        P(CTX),
        P(None, HEAD),
        P(None, HEAD),
        P(HEAD, CTX),
    )
    out_specs = P(CTX, HEAD)
    return jax.shard_map(body, mesh=fine, in_specs=in_specs, out_specs=out_specs, check_vma=False)
```

```python
import math

import jax
import jax.numpy as jnp
from jax import lax
from jax.experimental import pallas as pl
from jax.sharding import Mesh
from jax.sharding import PartitionSpec as P

LATENT = 512
ROPE = 64
NOPE = 128
VDIM = 128


masked_value = -1e30


def rope_tables(token_pos, width):
    half_width = width // 2
    freqs = jnp.exp(jnp.arange(half_width, dtype=jnp.float32) * (-2.0 * math.log(10000.0) / width))
    angle = token_pos.astype(jnp.float32)[:, None] * freqs[None, :]
    return (jnp.cos(angle), jnp.sin(angle))


def rotate(values, cosine, sine):
    half_width = values.shape[-1] // 2
    first_half = values[..., :half_width]
    second_half = values[..., half_width:]
    cos_part = cosine[:, None, :]
    sin_part = sine[:, None, :]
    return jnp.concatenate(
        [
            first_half * cos_part - second_half * sin_part,
            second_half * cos_part + first_half * sin_part,
        ],
        axis=-1,
    )


def attention_kernel(q_ref, qi_ref, ka_ref, ia_ref, kb_ref, ib_ref, v_ref, o_ref):
    scale = 1.0 / math.sqrt(NOPE + ROPE)
    queries = q_ref[...]
    query_index = qi_ref[...]

    def masked_scores(k_ref, i_ref):
        scores = lax.dot_general(
            queries, k_ref[...], (((1,), (1,)), ((), ())), preferred_element_type=jnp.float32
        )
        visible = i_ref[...] <= query_index
        return jnp.where(visible, scores * scale, masked_value), visible

    scores_a, visible_a = masked_scores(ka_ref, ia_ref)
    scores_b, visible_b = masked_scores(kb_ref, ib_ref)
    peak = jnp.maximum(
        jnp.max(scores_a, axis=1, keepdims=True), jnp.max(scores_b, axis=1, keepdims=True)
    )
    weights_a = jnp.where(visible_a, jnp.exp(scores_a - peak), 0.0)
    weights_b = jnp.where(visible_b, jnp.exp(scores_b - peak), 0.0)
    totals = jnp.sum(weights_a, axis=1, keepdims=True) + jnp.sum(weights_b, axis=1, keepdims=True)
    summed = jnp.dot(
        weights_a.astype(jnp.bfloat16), ka_ref[:, :LATENT], preferred_element_type=jnp.float32
    )
    summed = summed + jnp.dot(
        weights_b.astype(jnp.bfloat16), kb_ref[:, :LATENT], preferred_element_type=jnp.float32
    )
    latent_out = (summed / totals).astype(jnp.bfloat16)
    head_count = v_ref.shape[1] // VDIM
    tokens = latent_out.shape[0] // head_count
    for head in range(head_count):
        head_out = jnp.dot(
            latent_out[head * tokens : (head + 1) * tokens],
            v_ref[:, head * VDIM : (head + 1) * VDIM],
            preferred_element_type=jnp.float32,
        )
        o_ref[:, head * VDIM : (head + 1) * VDIM] = head_out.astype(jnp.bfloat16)


def attend(query_rows, query_index, halves, value_up):
    rows = query_rows.shape[0]
    operands = [query_rows, query_index.reshape(rows, 1)]
    key_count = 0
    for keys, key_index in halves:
        operands += [keys, key_index]
        key_count += keys.shape[0]
    width = query_rows.shape[1]
    cost = pl.CostEstimate(
        flops=2 * rows * key_count * (width + LATENT),
        transcendentals=rows * key_count,
        bytes_accessed=2 * (rows * width + key_count * width + rows * LATENT),
    )
    operands.append(value_up)
    tokens = rows * VDIM // value_up.shape[1]
    return pl.pallas_call(
        attention_kernel,
        out_shape=jax.ShapeDtypeStruct((tokens, value_up.shape[1]), jnp.bfloat16),
        cost_estimate=cost,
    )(*operands)


def exchange(acc, axis, size, bit, same_over_yh):
    pairs = [(i, i ^ bit) for i in range(size)]
    if axis != "yl" or not same_over_yh:
        return lax.ppermute(acc, axis, pairs)
    half = acc.shape[0] // 2
    near = lax.ppermute(acc[:half], "yl", pairs)
    far = lax.ppermute(acc[half:], ("yl", "yh"), [(i, i ^ 3) for i in range(4)])
    return jnp.concatenate([near, far], axis=0)


def gather_in_order(local, axes, same_over_yh):
    acc = local[None]
    for axis, size in axes:
        bit = size // 2
        while bit >= 1:
            upper = (lax.axis_index(axis) // bit) % 2 == 1
            other = exchange(acc, axis, size, bit, same_over_yh)
            first = jnp.where(upper, other, acc)
            second = jnp.where(upper, acc, other)
            acc = jnp.stack([first, second], axis=1).reshape((-1,) + local.shape)
            bit //= 2
    return acc.reshape((-1,) + local.shape[1:])


ABSENT = 1 << 20


def gather_earlier_keys(local):
    cubes = lax.axis_size("zh")
    cube = lax.axis_index("zh")
    within = lax.axis_index(("zl", "yl", "co"))
    per_cube = lax.axis_size(("zl", "yl", "co"))
    blocks = [local]
    for shift in range(1, cubes):
        blocks.append(lax.ppermute(local, "zh", [(i, i + shift) for i in range(cubes - shift)]))
    acc = jnp.stack(blocks)
    source = cube - jnp.arange(cubes, dtype=jnp.int32)
    index = jnp.where(source >= 0, source * per_cube + within, ABSENT)
    rounds = (("zl", 2), ("yl", 2), ("co", 2))
    for number, (axis, size) in enumerate(rounds):
        step = per_cube // size
        per_cube = step
        other = exchange(acc, axis, size, 1, True)
        other_index = jnp.where(index < ABSENT, index ^ step, ABSENT)
        if number == len(rounds) - 1:
            return (acc, index), (other, other_index)
        acc = jnp.concatenate([acc, other], axis=0)
        index = jnp.concatenate([index, other_index])


def scatter_sum(blocks):
    rows = lax.axis_size("yh")
    columns = lax.axis_size("x")
    x = lax.axis_index("x")
    yh = lax.axis_index("yh")
    blocks = blocks.reshape((columns, rows) + blocks.shape[1:])
    row_sums = blocks[x]
    for shift in range(1, columns):
        sent = blocks[x ^ shift].astype(jnp.bfloat16)
        row_sums = row_sums + lax.ppermute(
            sent, "x", [(i, i ^ shift) for i in range(columns)]
        ).astype(jnp.float32)
    total = row_sums[yh]
    for shift in range(1, rows):
        sent = row_sums[yh ^ shift].astype(jnp.bfloat16)
        total = total + lax.ppermute(
            sent, "yh", [(i, i ^ shift) for i in range(rows)]
        ).astype(jnp.float32)
    return total


def body(queries_nope, queries_rope, latents, rope_keys, positions, key_up, value_up, out_proj):
    token_count = latents.shape[0]
    head_count = key_up.shape[1] // NOPE
    cosine, sine = rope_tables(positions, ROPE)
    rot_queries = rotate(
        queries_rope.astype(jnp.float32).reshape(token_count, head_count, ROPE), cosine, sine
    ).astype(jnp.bfloat16)
    rot_keys = rotate(rope_keys.astype(jnp.float32)[:, None, :], cosine, sine)[:, 0, :].astype(
        jnp.bfloat16
    )
    lat_queries = jnp.einsum(
        "thn,lhn->thl",
        queries_nope.reshape(token_count, head_count, NOPE),
        key_up.reshape(LATENT, head_count, NOPE),
        preferred_element_type=jnp.float32,
    ).astype(jnp.bfloat16)
    query_rows = (
        jnp.concatenate([lat_queries, rot_queries], axis=-1)
        .transpose(1, 0, 2)
        .reshape(head_count * token_count, LATENT + ROPE)
    )
    local_keys = jnp.concatenate([latents, rot_keys], axis=-1)
    halves = []
    for key_blocks, block_index in gather_earlier_keys(local_keys):
        keys = key_blocks.reshape(-1, LATENT + ROPE)
        key_index = (
            block_index[:, None] * token_count + jnp.arange(token_count, dtype=jnp.int32)[None, :]
        ).reshape(1, -1)
        halves.append((keys, key_index))
    first_token = lax.axis_index(CTX) * token_count
    query_index = jnp.tile(first_token + jnp.arange(token_count, dtype=jnp.int32), head_count)
    head_out = attend(query_rows, query_index, halves, value_up)
    pair = gather_in_order(out_proj.T, (("yl", 2),), False)
    pair = pair.reshape(2, out_proj.shape[1], -1).transpose(2, 0, 1).reshape(out_proj.shape[0], -1)
    own = lax.all_gather(pair, ("zh", "zl"), axis=1, tiled=True)
    own, _ = lax.optimization_barrier((own, halves[1][0]))
    swapped = lax.ppermute(own, "co", [(0, 1), (1, 0)])
    upper = lax.axis_index("co") == 1
    groups = lax.axis_size(HEAD)
    halves = [
        jnp.dot(head_out, half, preferred_element_type=jnp.float32).reshape(token_count, groups, -1)
        for half in (own, swapped)
    ]
    partial_sums = jnp.concatenate(halves, axis=2).transpose(1, 0, 2)
    mine = scatter_sum(partial_sums)
    half_width = mine.shape[1] // 2
    mine = jnp.where(
        upper,
        jnp.concatenate([mine[:, half_width:], mine[:, :half_width]], axis=1),
        mine,
    )
    width = out_proj.shape[1]
    mine = mine.reshape(token_count, 2, -1, width).transpose(0, 2, 1, 3)
    return mine.reshape(token_count, -1).astype(jnp.bfloat16)


CTX_SPLIT = (("zh", 8), ("zl", 2), ("yl", 2), ("co", 2))
HEAD_SPLIT = (("x", 4), ("yh", 2))
CTX = tuple(name for name, _ in CTX_SPLIT)
HEAD = tuple(name for name, _ in HEAD_SPLIT)


def solution(mesh):
    sizes = tuple(size for _, size in CTX_SPLIT + HEAD_SPLIT)
    fine = Mesh(mesh.devices.reshape(sizes), CTX + HEAD)
    in_specs = (
        P(CTX, HEAD),
        P(CTX, HEAD),
        P(CTX, None),
        P(CTX, None),
        P(CTX),
        P(None, HEAD),
        P(None, HEAD),
        P(HEAD, CTX),
    )
    out_specs = P(CTX, HEAD)
    return jax.shard_map(body, mesh=fine, in_specs=in_specs, out_specs=out_specs, check_vma=False)
```

```python
import math

import jax
import jax.numpy as jnp
from jax import lax
from jax.experimental import pallas as pl
from jax.sharding import Mesh
from jax.sharding import PartitionSpec as P

LATENT = 512
ROPE = 64
NOPE = 128
VDIM = 128


masked_value = -1e30


def rope_tables(token_pos, width):
    half_width = width // 2
    freqs = jnp.exp(jnp.arange(half_width, dtype=jnp.float32) * (-2.0 * math.log(10000.0) / width))
    angle = token_pos.astype(jnp.float32)[:, None] * freqs[None, :]
    return (jnp.cos(angle), jnp.sin(angle))


def rotate(values, cosine, sine):
    half_width = values.shape[-1] // 2
    first_half = values[..., :half_width]
    second_half = values[..., half_width:]
    cos_part = cosine[:, None, :]
    sin_part = sine[:, None, :]
    return jnp.concatenate(
        [
            first_half * cos_part - second_half * sin_part,
            second_half * cos_part + first_half * sin_part,
        ],
        axis=-1,
    )


def attention_kernel(q_ref, qi_ref, ka_ref, ia_ref, kb_ref, ib_ref, v_ref, o_ref):
    scale = 1.0 / math.sqrt(NOPE + ROPE)
    queries = q_ref[...]
    query_index = qi_ref[...]

    def masked_scores(k_ref, i_ref):
        scores = lax.dot_general(
            queries, k_ref[...], (((1,), (1,)), ((), ())), preferred_element_type=jnp.float32
        )
        visible = i_ref[...] <= query_index
        return jnp.where(visible, scores * scale, masked_value), visible

    scores_a, visible_a = masked_scores(ka_ref, ia_ref)
    scores_b, visible_b = masked_scores(kb_ref, ib_ref)
    peak = jnp.maximum(
        jnp.max(scores_a, axis=1, keepdims=True), jnp.max(scores_b, axis=1, keepdims=True)
    )
    weights_a = jnp.where(visible_a, jnp.exp(scores_a - peak), 0.0)
    weights_b = jnp.where(visible_b, jnp.exp(scores_b - peak), 0.0)
    totals = jnp.sum(weights_a, axis=1, keepdims=True) + jnp.sum(weights_b, axis=1, keepdims=True)
    summed = jnp.dot(
        weights_a.astype(jnp.bfloat16), ka_ref[:, :LATENT], preferred_element_type=jnp.float32
    )
    summed = summed + jnp.dot(
        weights_b.astype(jnp.bfloat16), kb_ref[:, :LATENT], preferred_element_type=jnp.float32
    )
    latent_out = (summed / totals).astype(jnp.bfloat16)
    head_count = v_ref.shape[1] // VDIM
    tokens = latent_out.shape[0] // head_count
    for head in range(head_count):
        head_out = jnp.dot(
            latent_out[head * tokens : (head + 1) * tokens],
            v_ref[:, head * VDIM : (head + 1) * VDIM],
            preferred_element_type=jnp.float32,
        )
        o_ref[:, head * VDIM : (head + 1) * VDIM] = head_out.astype(jnp.bfloat16)


def attend(query_rows, query_index, halves, value_up):
    rows = query_rows.shape[0]
    operands = [query_rows, query_index.reshape(rows, 1)]
    key_count = 0
    for keys, key_index in halves:
        operands += [keys, key_index]
        key_count += keys.shape[0]
    width = query_rows.shape[1]
    cost = pl.CostEstimate(
        flops=2 * rows * key_count * (width + LATENT),
        transcendentals=rows * key_count,
        bytes_accessed=2 * (rows * width + key_count * width + rows * LATENT),
    )
    operands.append(value_up)
    tokens = rows * VDIM // value_up.shape[1]
    return pl.pallas_call(
        attention_kernel,
        out_shape=jax.ShapeDtypeStruct((tokens, value_up.shape[1]), jnp.bfloat16),
        cost_estimate=cost,
    )(*operands)


def exchange(acc, axis, size, bit, same_over_yh):
    pairs = [(i, i ^ bit) for i in range(size)]
    if axis != "yl" or not same_over_yh:
        return lax.ppermute(acc, axis, pairs)
    half = acc.shape[0] // 2
    near = lax.ppermute(acc[:half], "yl", pairs)
    far = lax.ppermute(acc[half:], ("yl", "yh"), [(i, i ^ 3) for i in range(4)])
    return jnp.concatenate([near, far], axis=0)


def gather_in_order(local, axes, same_over_yh):
    acc = local[None]
    for axis, size in axes:
        bit = size // 2
        while bit >= 1:
            upper = (lax.axis_index(axis) // bit) % 2 == 1
            other = exchange(acc, axis, size, bit, same_over_yh)
            first = jnp.where(upper, other, acc)
            second = jnp.where(upper, acc, other)
            acc = jnp.stack([first, second], axis=1).reshape((-1,) + local.shape)
            bit //= 2
    return acc.reshape((-1,) + local.shape[1:])


ABSENT = 1 << 20


def gather_earlier_keys(local):
    cubes = lax.axis_size("zh")
    cube = lax.axis_index("zh")
    within = lax.axis_index(("zl", "yl", "co"))
    per_cube = lax.axis_size(("zl", "yl", "co"))
    sent = {}
    for shift in sorted(range(1, cubes), key=lambda d: -min(d, cubes - d)):
        sent[shift] = lax.ppermute(local, "zh", [(i, i + shift) for i in range(cubes - shift)])
    acc = jnp.stack([local] + [sent[shift] for shift in range(1, cubes)])
    source = cube - jnp.arange(cubes, dtype=jnp.int32)
    index = jnp.where(source >= 0, source * per_cube + within, ABSENT)
    rounds = (("zl", 2), ("yl", 2), ("co", 2))
    for number, (axis, size) in enumerate(rounds):
        step = per_cube // size
        per_cube = step
        other = exchange(acc, axis, size, 1, True)
        other_index = jnp.where(index < ABSENT, index ^ step, ABSENT)
        if number == len(rounds) - 1:
            return (acc, index), (other, other_index)
        acc = jnp.concatenate([acc, other], axis=0)
        index = jnp.concatenate([index, other_index])


def scatter_sum(blocks):
    rows = lax.axis_size("yh")
    columns = lax.axis_size("x")
    x = lax.axis_index("x")
    yh = lax.axis_index("yh")
    blocks = blocks.reshape((columns, rows) + blocks.shape[1:])
    row_sums = blocks[x]
    for shift in range(1, columns):
        sent = blocks[x ^ shift].astype(jnp.bfloat16)
        row_sums = row_sums + lax.ppermute(
            sent, "x", [(i, i ^ shift) for i in range(columns)]
        ).astype(jnp.float32)
    total = row_sums[yh]
    for shift in range(1, rows):
        sent = row_sums[yh ^ shift].astype(jnp.bfloat16)
        total = total + lax.ppermute(
            sent, "yh", [(i, i ^ shift) for i in range(rows)]
        ).astype(jnp.float32)
    return total


def body(queries_nope, queries_rope, latents, rope_keys, positions, key_up, value_up, out_proj):
    token_count = latents.shape[0]
    head_count = key_up.shape[1] // NOPE
    cosine, sine = rope_tables(positions, ROPE)
    rot_queries = rotate(
        queries_rope.astype(jnp.float32).reshape(token_count, head_count, ROPE), cosine, sine
    ).astype(jnp.bfloat16)
    rot_keys = rotate(rope_keys.astype(jnp.float32)[:, None, :], cosine, sine)[:, 0, :].astype(
        jnp.bfloat16
    )
    lat_queries = jnp.einsum(
        "thn,lhn->thl",
        queries_nope.reshape(token_count, head_count, NOPE),
        key_up.reshape(LATENT, head_count, NOPE),
        preferred_element_type=jnp.float32,
    ).astype(jnp.bfloat16)
    query_rows = (
        jnp.concatenate([lat_queries, rot_queries], axis=-1)
        .transpose(1, 0, 2)
        .reshape(head_count * token_count, LATENT + ROPE)
    )
    local_keys = jnp.concatenate([latents, rot_keys], axis=-1)
    halves = []
    for key_blocks, block_index in gather_earlier_keys(local_keys):
        keys = key_blocks.reshape(-1, LATENT + ROPE)
        key_index = (
            block_index[:, None] * token_count + jnp.arange(token_count, dtype=jnp.int32)[None, :]
        ).reshape(1, -1)
        halves.append((keys, key_index))
    first_token = lax.axis_index(CTX) * token_count
    query_index = jnp.tile(first_token + jnp.arange(token_count, dtype=jnp.int32), head_count)
    head_out = attend(query_rows, query_index, halves, value_up)
    pair = gather_in_order(out_proj.T, (("yl", 2),), False)
    pair = pair.reshape(2, out_proj.shape[1], -1).transpose(2, 0, 1).reshape(out_proj.shape[0], -1)
    own = lax.all_gather(pair, ("zh", "zl"), axis=1, tiled=True)
    swapped = lax.ppermute(own, "co", [(0, 1), (1, 0)])
    upper = lax.axis_index("co") == 1
    groups = lax.axis_size(HEAD)
    halves = [
        jnp.dot(head_out, half, preferred_element_type=jnp.float32).reshape(token_count, groups, -1)
        for half in (own, swapped)
    ]
    partial_sums = jnp.concatenate(halves, axis=2).transpose(1, 0, 2)
    mine = scatter_sum(partial_sums)
    half_width = mine.shape[1] // 2
    mine = jnp.where(
        upper,
        jnp.concatenate([mine[:, half_width:], mine[:, :half_width]], axis=1),
        mine,
    )
    width = out_proj.shape[1]
    mine = mine.reshape(token_count, 2, -1, width).transpose(0, 2, 1, 3)
    return mine.reshape(token_count, -1).astype(jnp.bfloat16)


CTX_SPLIT = (("zh", 8), ("zl", 2), ("yl", 2), ("co", 2))
HEAD_SPLIT = (("x", 4), ("yh", 2))
CTX = tuple(name for name, _ in CTX_SPLIT)
HEAD = tuple(name for name, _ in HEAD_SPLIT)


def solution(mesh):
    sizes = tuple(size for _, size in CTX_SPLIT + HEAD_SPLIT)
    fine = Mesh(mesh.devices.reshape(sizes), CTX + HEAD)
    in_specs = (
        P(CTX, HEAD),
        P(CTX, HEAD),
        P(CTX, None),
        P(CTX, None),
        P(CTX),
        P(None, HEAD),
        P(None, HEAD),
        P(HEAD, CTX),
    )
    out_specs = P(CTX, HEAD)
    return jax.shard_map(body, mesh=fine, in_specs=in_specs, out_specs=out_specs, check_vma=False)
```

```python
import math

import jax
import jax.numpy as jnp
from jax import lax
from jax.experimental import pallas as pl
from jax.sharding import Mesh
from jax.sharding import PartitionSpec as P

LATENT = 512
ROPE = 64
NOPE = 128
VDIM = 128


masked_value = -1e30


def rope_tables(token_pos, width):
    half_width = width // 2
    freqs = jnp.exp(jnp.arange(half_width, dtype=jnp.float32) * (-2.0 * math.log(10000.0) / width))
    angle = token_pos.astype(jnp.float32)[:, None] * freqs[None, :]
    return (jnp.cos(angle), jnp.sin(angle))


def rotate(values, cosine, sine):
    half_width = values.shape[-1] // 2
    first_half = values[..., :half_width]
    second_half = values[..., half_width:]
    cos_part = cosine[:, None, :]
    sin_part = sine[:, None, :]
    return jnp.concatenate(
        [
            first_half * cos_part - second_half * sin_part,
            second_half * cos_part + first_half * sin_part,
        ],
        axis=-1,
    )


def attention_kernel(q_ref, qi_ref, ka_ref, ia_ref, kb_ref, ib_ref, v_ref, o_ref):
    scale = 1.0 / math.sqrt(NOPE + ROPE)
    queries = q_ref[...]
    query_index = qi_ref[...]

    def masked_scores(k_ref, i_ref):
        scores = lax.dot_general(
            queries, k_ref[...], (((1,), (1,)), ((), ())), preferred_element_type=jnp.float32
        )
        visible = i_ref[...] <= query_index
        return jnp.where(visible, scores * scale, masked_value), visible

    scores_a, visible_a = masked_scores(ka_ref, ia_ref)
    scores_b, visible_b = masked_scores(kb_ref, ib_ref)
    peak = jnp.maximum(
        jnp.max(scores_a, axis=1, keepdims=True), jnp.max(scores_b, axis=1, keepdims=True)
    )
    weights_a = jnp.where(visible_a, jnp.exp(scores_a - peak), 0.0)
    weights_b = jnp.where(visible_b, jnp.exp(scores_b - peak), 0.0)
    totals = jnp.sum(weights_a, axis=1, keepdims=True) + jnp.sum(weights_b, axis=1, keepdims=True)
    summed = jnp.dot(
        weights_a.astype(jnp.bfloat16), ka_ref[:, :LATENT], preferred_element_type=jnp.float32
    )
    summed = summed + jnp.dot(
        weights_b.astype(jnp.bfloat16), kb_ref[:, :LATENT], preferred_element_type=jnp.float32
    )
    latent_out = (summed / totals).astype(jnp.bfloat16)
    head_count = v_ref.shape[1] // VDIM
    tokens = latent_out.shape[0] // head_count
    for head in range(head_count):
        head_out = jnp.dot(
            latent_out[head * tokens : (head + 1) * tokens],
            v_ref[:, head * VDIM : (head + 1) * VDIM],
            preferred_element_type=jnp.float32,
        )
        o_ref[:, head * VDIM : (head + 1) * VDIM] = head_out.astype(jnp.bfloat16)


def attend(query_rows, query_index, halves, value_up):
    rows = query_rows.shape[0]
    operands = [query_rows, query_index.reshape(rows, 1)]
    key_count = 0
    for keys, key_index in halves:
        operands += [keys, key_index]
        key_count += keys.shape[0]
    width = query_rows.shape[1]
    cost = pl.CostEstimate(
        flops=2 * rows * key_count * (width + LATENT),
        transcendentals=rows * key_count,
        bytes_accessed=2 * (rows * width + key_count * width + rows * LATENT),
    )
    operands.append(value_up)
    tokens = rows * VDIM // value_up.shape[1]
    return pl.pallas_call(
        attention_kernel,
        out_shape=jax.ShapeDtypeStruct((tokens, value_up.shape[1]), jnp.bfloat16),
        cost_estimate=cost,
    )(*operands)


def exchange(acc, axis, size, bit, same_over_yh):
    pairs = [(i, i ^ bit) for i in range(size)]
    if axis != "yl" or not same_over_yh:
        return lax.ppermute(acc, axis, pairs)
    half = acc.shape[0] // 2
    near = lax.ppermute(acc[:half], "yl", pairs)
    far = lax.ppermute(acc[half:], ("yl", "yh"), [(i, i ^ 3) for i in range(4)])
    return jnp.concatenate([near, far], axis=0)


def gather_in_order(local, axes, same_over_yh):
    acc = local[None]
    for axis, size in axes:
        bit = size // 2
        while bit >= 1:
            upper = (lax.axis_index(axis) // bit) % 2 == 1
            other = exchange(acc, axis, size, bit, same_over_yh)
            first = jnp.where(upper, other, acc)
            second = jnp.where(upper, acc, other)
            acc = jnp.stack([first, second], axis=1).reshape((-1,) + local.shape)
            bit //= 2
    return acc.reshape((-1,) + local.shape[1:])


ABSENT = 1 << 20


def gather_earlier_keys(local):
    cubes = lax.axis_size("zh")
    cube = lax.axis_index("zh")
    within = lax.axis_index(("zl", "yl", "co"))
    per_cube = lax.axis_size(("zl", "yl", "co"))
    sent = {}
    for shift in sorted(range(1, cubes), key=lambda d: -min(d, cubes - d)):
        sent[shift] = lax.ppermute(local, "zh", [(i, i + shift) for i in range(cubes - shift)])
    acc = jnp.stack([local] + [sent[shift] for shift in range(1, cubes)])
    source = cube - jnp.arange(cubes, dtype=jnp.int32)
    index = jnp.where(source >= 0, source * per_cube + within, ABSENT)
    rounds = (("zl", 2), ("yl", 2), ("co", 2))
    for number, (axis, size) in enumerate(rounds):
        step = per_cube // size
        per_cube = step
        other = exchange(acc, axis, size, 1, True)
        other_index = jnp.where(index < ABSENT, index ^ step, ABSENT)
        if number == len(rounds) - 1:
            return (acc, index), (other, other_index)
        acc = jnp.concatenate([acc, other], axis=0)
        index = jnp.concatenate([index, other_index])


def scatter_sum(blocks):
    rows = lax.axis_size("yh")
    columns = lax.axis_size("x")
    x = lax.axis_index("x")
    yh = lax.axis_index("yh")
    blocks = blocks.reshape((columns, rows) + blocks.shape[1:])
    row_sums = blocks[x]
    for shift in sorted(range(1, columns), key=lambda d: -bin(d).count("0")):
        sent = blocks[x ^ shift].astype(jnp.bfloat16)
        row_sums = row_sums + lax.ppermute(
            sent, "x", [(i, i ^ shift) for i in range(columns)]
        ).astype(jnp.float32)
    total = row_sums[yh]
    for shift in range(1, rows):
        sent = row_sums[yh ^ shift].astype(jnp.bfloat16)
        total = total + lax.ppermute(
            sent, "yh", [(i, i ^ shift) for i in range(rows)]
        ).astype(jnp.float32)
    return total


def body(queries_nope, queries_rope, latents, rope_keys, positions, key_up, value_up, out_proj):
    token_count = latents.shape[0]
    head_count = key_up.shape[1] // NOPE
    cosine, sine = rope_tables(positions, ROPE)
    rot_queries = rotate(
        queries_rope.astype(jnp.float32).reshape(token_count, head_count, ROPE), cosine, sine
    ).astype(jnp.bfloat16)
    rot_keys = rotate(rope_keys.astype(jnp.float32)[:, None, :], cosine, sine)[:, 0, :].astype(
        jnp.bfloat16
    )
    lat_queries = jnp.einsum(
        "thn,lhn->thl",
        queries_nope.reshape(token_count, head_count, NOPE),
        key_up.reshape(LATENT, head_count, NOPE),
        preferred_element_type=jnp.float32,
    ).astype(jnp.bfloat16)
    query_rows = (
        jnp.concatenate([lat_queries, rot_queries], axis=-1)
        .transpose(1, 0, 2)
        .reshape(head_count * token_count, LATENT + ROPE)
    )
    local_keys = jnp.concatenate([latents, rot_keys], axis=-1)
    halves = []
    for key_blocks, block_index in gather_earlier_keys(local_keys):
        keys = key_blocks.reshape(-1, LATENT + ROPE)
        key_index = (
            block_index[:, None] * token_count + jnp.arange(token_count, dtype=jnp.int32)[None, :]
        ).reshape(1, -1)
        halves.append((keys, key_index))
    first_token = lax.axis_index(CTX) * token_count
    query_index = jnp.tile(first_token + jnp.arange(token_count, dtype=jnp.int32), head_count)
    head_out = attend(query_rows, query_index, halves, value_up)
    pair = gather_in_order(out_proj.T, (("yl", 2),), False)
    pair = pair.reshape(2, out_proj.shape[1], -1).transpose(2, 0, 1).reshape(out_proj.shape[0], -1)
    own = lax.all_gather(pair, ("zh", "zl"), axis=1, tiled=True)
    swapped = lax.ppermute(own, "co", [(0, 1), (1, 0)])
    upper = lax.axis_index("co") == 1
    groups = lax.axis_size(HEAD)
    halves = [
        jnp.dot(head_out, half, preferred_element_type=jnp.float32).reshape(token_count, groups, -1)
        for half in (own, swapped)
    ]
    partial_sums = jnp.concatenate(halves, axis=2).transpose(1, 0, 2)
    mine = scatter_sum(partial_sums)
    half_width = mine.shape[1] // 2
    mine = jnp.where(
        upper,
        jnp.concatenate([mine[:, half_width:], mine[:, :half_width]], axis=1),
        mine,
    )
    width = out_proj.shape[1]
    mine = mine.reshape(token_count, 2, -1, width).transpose(0, 2, 1, 3)
    return mine.reshape(token_count, -1).astype(jnp.bfloat16)


CTX_SPLIT = (("zh", 8), ("zl", 2), ("yl", 2), ("co", 2))
HEAD_SPLIT = (("x", 4), ("yh", 2))
CTX = tuple(name for name, _ in CTX_SPLIT)
HEAD = tuple(name for name, _ in HEAD_SPLIT)


def solution(mesh):
    sizes = tuple(size for _, size in CTX_SPLIT + HEAD_SPLIT)
    fine = Mesh(mesh.devices.reshape(sizes), CTX + HEAD)
    in_specs = (
        P(CTX, HEAD),
        P(CTX, HEAD),
        P(CTX, None),
        P(CTX, None),
        P(CTX),
        P(None, HEAD),
        P(None, HEAD),
        P(HEAD, CTX),
    )
    out_specs = P(CTX, HEAD)
    return jax.shard_map(body, mesh=fine, in_specs=in_specs, out_specs=out_specs, check_vma=False)
```
